512 devices in a mesh: pos: 64 (over z, y), mode: 8 (over x, core).
Axes of the slice: x: 4, y: 4, z: 16, core: 2. Of those that a mesh axis runs over, the one named last changes fastest.
Arguments:
- object_field: float32 [2, 8192, 512], P(None, 'pos'), may hold values from -6 to 6
- probe: float32 [2, 8, 256, 256], P(None, 'mode'), may hold values from -3 to 3
- measured: float32 [192, 256, 256], P('pos'), may hold values from 0 to 16
- row_offsets: int32 [192], P('pos'), may hold values from 0 to 127
- col_offsets: int32 [192], P('pos'), may hold values from 0 to 256
- tile_counts: int32 [64], P('pos'), may hold values from 1 to 3, 96 in all
Outputs:
- updated_object: float32 [2, 8192, 512], P(None, ('pos', 'mode'))
The draws below stay inside these ranges and needn't reach their ends.
Inputs may be any that keep to these rules, and one draw needn't show every extreme that they name: Slots 0 to tile_counts[t] - 1 of tile t hold scan positions, the others are empty; the counts sum to 96 and the largest equals 3.
All inputs are finite; a program needn't handle non-finite values. No bound on the sum of `tile_counts` on one device may be relied on, other than what follows from the above.
Results may differ from the reference program's by a relative error of at most 0.0016.
Values sent between devices are 32-bit elements; how exact they have to be, the bound alone decides.
No kernel may reach another device: no remote copies, remote signals or barrier semaphores. Data moves between devices by JAX's collectives and lax.ppermute only.
A program may use at most 64 MiB of HBM per device.

```python
import math
import jax
import jax.numpy as jnp
import numpy as np
from jax import lax

PAT = 256
MODES = 8
TILE_H = 128
OBJ_W = 512
SLOTS = 3
TILES = 64
OBJ_H = 8192
POSITIONS = 192
LIVE = 96


def set_ends(entries, stream_key, low, high):
    longest = entries.shape.index(max(entries.shape))
    spots = []
    for shift in (0, 1):
        where = [jax.random.randint(jax.random.fold_in(stream_key, axis), (), 0, length) for axis, length in enumerate(entries.shape)]
        where[longest] = (where[longest] + shift) % entries.shape[longest]
        spots.append(tuple(where))
    return entries.at[spots[0]].set(low).at[spots[1]].set(high)


def block_scale(own_key, shape, pieces, low, high):
    loudness, own = 1.0, jax.random.fold_in(own_key, 6)
    for dim, blocks in pieces:
        heights = jnp.exp(jax.random.uniform(jax.random.fold_in(own, dim), (blocks,), jnp.float32, low / len(pieces), high / len(pieces)))
        loudness = loudness * jnp.repeat(heights, shape[dim] // blocks).reshape([-1 if axis == dim else 1 for axis in range(len(shape))])
    return loudness


def split_up(amount, total, limit, lean):
    weights = [(1 << 20) // math.isqrt(rank ** lean) + 1 for rank in range(2, amount + 1)]
    spare, given = total - limit - (amount - 1), [1] * (amount - 1)
    while spare > 0:
        candidates = [i for i in range(amount - 1) if given[i] < limit]
        mass, left = sum([weights[i] for i in candidates]), spare
        for i in candidates:
            more = min(limit - given[i], max(1, left * weights[i] // mass), spare)
            given[i] = given[i] + more
            spare = spare - more
    return np.array([limit] + given)


def ragged_sizes(key, count, total, limit, lean):
    if count == 2:
        one = jax.random.randint(key, (), max(1, total - limit), min(limit, total - 1) + 1)
        return jnp.stack([one, total - one])
    tallies = jnp.asarray(split_up(count, total, limit, lean), jnp.int32)
    twos = (count - 1) // 2
    giver, taker = tallies[1:1 + 2 * twos:2], tallies[2:2 + 2 * twos:2]
    slack = jnp.minimum(giver - 1, limit - taker)
    passed = jax.random.randint(jax.random.fold_in(key, 1), (twos,), 0, 1 << 20) % (slack + 1)
    tallies = tallies.at[1:1 + 2 * twos:2].set(giver - passed).at[2:2 + 2 * twos:2].set(taker + passed)
    return tallies[jax.random.permutation(jax.random.fold_in(key, 2), count)]


def noise(stream_key, extent, width, limit, shards=(), kind=jnp.bfloat16):
    factor_of = block_scale(stream_key, extent, shards, -0.22, 0.18) if shards else 1.0
    values = jax.random.normal(stream_key, extent, jnp.float32) * width * factor_of
    return jnp.minimum(jnp.maximum(values, -limit), limit).astype(kind)


def setup_inputs(seed: int = 0) -> dict:
    seeds = jax.random.split(jax.random.key(seed), 7)
    return {
        "object_field": noise(seeds[0], (2, OBJ_H, OBJ_W), 1.0, 6.0, ((1, 64),), jnp.float32),
        "probe": noise(seeds[1], (2, MODES, PAT, PAT), 0.5, 3.0, ((1, 8),), jnp.float32),
        "measured": jnp.clip(16.0 * jax.random.uniform(seeds[2], (POSITIONS, PAT, PAT), jnp.float32) ** block_scale(seeds[2], (POSITIONS, PAT, PAT), ((0, 64),), -0.2, 0.2), 0.0, 16.0),
        "row_offsets": set_ends(jax.random.randint(seeds[3], (POSITIONS,), 0, TILE_H), jax.random.fold_in(seeds[3], 1), 0, TILE_H - 1).astype(jnp.int32),
        "col_offsets": set_ends(jax.random.randint(seeds[4], (POSITIONS,), 0, OBJ_W - PAT + 1), jax.random.fold_in(seeds[4], 1), 0, OBJ_W - PAT).astype(jnp.int32),
        "tile_counts": ragged_sizes(seeds[5], TILES, LIVE, SLOTS, 2).astype(jnp.int32),
    }


def dft_tables(pattern):
    counter = jnp.arange(pattern, dtype=jnp.int32)
    phases = counter[:, None] * counter[None, :] % pattern
    angles = phases.astype(jnp.float32) * (2.0 * math.pi / pattern)
    factor = 1.0 / math.sqrt(pattern)
    return ((jnp.cos(angles) * factor).astype(jnp.bfloat16), (-jnp.sin(angles) * factor).astype(jnp.bfloat16))

def reference(object_field, probe, measured, row_offsets, col_offsets, tile_counts):
    real_table, imag_table = dft_tables(PAT)
    real_wide = real_table.astype(jnp.float32)
    imag_wide = imag_table.astype(jnp.float32)
    padded = jnp.pad(object_field, ((0, 0), (TILE_H, TILE_H), (0, 0)))
    probe_re = probe[0]
    probe_im = probe[1]
    probe_power = lax.optimization_barrier(jnp.sum(probe_re * probe_re + probe_im * probe_im, axis=0))
    anchor = jnp.zeros((), jnp.int32)

    def one_position(position, buffer):
        position = jnp.asarray(position).astype(jnp.int32)
        tile_id = position // SLOTS
        is_live = position % SLOTS < tile_counts[tile_id].astype(jnp.int32)
        top_row = (tile_id * TILE_H + TILE_H + row_offsets[position].astype(jnp.int32) - PAT // 2).astype(jnp.int32)
        column = col_offsets[position].astype(jnp.int32)
        window = lax.dynamic_slice(padded, (anchor, top_row, column), (2, PAT, PAT))
        exit_re = (probe_re * window[0] - probe_im * window[1]).astype(jnp.bfloat16)
        exit_im = (probe_re * window[1] + probe_im * window[0]).astype(jnp.bfloat16)
        wide_re = exit_re.astype(jnp.float32)
        wide_im = exit_im.astype(jnp.float32)
        half_re = (jnp.einsum('ua,kab->kub', real_wide, wide_re) - jnp.einsum('ua,kab->kub', imag_wide, wide_im)).astype(jnp.bfloat16).astype(jnp.float32)
        half_im = (jnp.einsum('ua,kab->kub', real_wide, wide_im) + jnp.einsum('ua,kab->kub', imag_wide, wide_re)).astype(jnp.bfloat16).astype(jnp.float32)
        wave_re = jnp.einsum('kub,bv->kuv', half_re, real_wide) - jnp.einsum('kub,bv->kuv', half_im, imag_wide)
        wave_im = jnp.einsum('kub,bv->kuv', half_re, imag_wide) + jnp.einsum('kub,bv->kuv', half_im, real_wide)
        model_power = lax.optimization_barrier(jnp.sum(wave_re * wave_re + wave_im * wave_im, axis=0))
        scaling = jnp.sqrt(measured[position]) / jnp.maximum(jnp.sqrt(model_power), 1.0)
        fixed_re = (scaling * wave_re).astype(jnp.bfloat16).astype(jnp.float32)
        fixed_im = (scaling * wave_im).astype(jnp.bfloat16).astype(jnp.float32)
        back_re = (jnp.einsum('ua,kab->kub', real_wide, fixed_re) + jnp.einsum('ua,kab->kub', imag_wide, fixed_im)).astype(jnp.bfloat16).astype(jnp.float32)
        back_im = (jnp.einsum('ua,kab->kub', real_wide, fixed_im) - jnp.einsum('ua,kab->kub', imag_wide, fixed_re)).astype(jnp.bfloat16).astype(jnp.float32)
        delta_re = jnp.einsum('kub,bv->kuv', back_re, real_wide) + jnp.einsum('kub,bv->kuv', back_im, imag_wide) - wide_re
        delta_im = jnp.einsum('kub,bv->kuv', back_im, real_wide) - jnp.einsum('kub,bv->kuv', back_re, imag_wide) - wide_im
        numer_re = lax.optimization_barrier(jnp.sum(probe_re * delta_re + probe_im * delta_im, axis=0))
        numer_im = lax.optimization_barrier(jnp.sum(probe_re * delta_im - probe_im * delta_re, axis=0))
        contrib = jnp.stack([numer_re, numer_im, probe_power])
        contrib = jnp.where(is_live, contrib, jnp.zeros_like(contrib))
        corner = (anchor, top_row, column)
        current = lax.dynamic_slice(buffer, corner, (3, PAT, PAT))
        return lax.dynamic_update_slice(buffer, current + contrib, corner)
    buffer = jnp.zeros((3, OBJ_H + 2 * TILE_H, OBJ_W), jnp.float32)
    buffer = lax.fori_loop(0, POSITIONS, one_position, buffer)
    inner = buffer[:, TILE_H:TILE_H + OBJ_H]
    return object_field + inner[:2] / (inner[2] + 1.0)
```

```python
import math

import jax
import jax.numpy as jnp
from jax import lax
from jax.experimental import pallas as pl
from jax.experimental.pallas import tpu as pltpu
from jax.sharding import PartitionSpec as P


def dft_tables(pattern):
    counter = jnp.arange(pattern, dtype=jnp.int32)
    phases = counter[:, None] * counter[None, :] % pattern
    angles = phases.astype(jnp.float32) * (2.0 * math.pi / pattern)
    factor = 1.0 / math.sqrt(pattern)
    return (
        (jnp.cos(angles) * factor).astype(jnp.bfloat16),
        (-jnp.sin(angles) * factor).astype(jnp.bfloat16),
    )


def neighbour_pairs(size, step):
    if step > 0:
        return [(i, i + 1) for i in range(size - 1)]
    return [(i + 1, i) for i in range(size - 1)]


def allreduce_mode(x):
    n = lax.axis_size("mode")
    d = 1
    while d < n:
        x = x + lax.ppermute(x, "mode", [(i, i ^ d) for i in range(n)])
        d *= 2
    return x


def reduce_scatter_mode(x):
    n = lax.axis_size("mode")
    k = n.bit_length() - 1
    m = lax.axis_index("mode")
    c, rows, w = x.shape
    x = x.reshape((c,) + (2,) * k + (rows // n, w))
    for i in range(k):
        d = 1 << i
        dim = k - i
        bit = (m // d) % 2
        keep = lax.dynamic_index_in_dim(x, bit, axis=dim, keepdims=False)
        send = lax.dynamic_index_in_dim(x, 1 - bit, axis=dim, keepdims=False)
        x = keep + lax.ppermute(send, "mode", [(j, j ^ d) for j in range(n)])
    return x.reshape(c, rows // n, w)


def _dot(a, b):
    return jnp.dot(a, b, preferred_element_type=jnp.float32)


def forward_kernel(roff, coff, cnt, ext_ref, probe_ref, fr_ref, fi_ref, exit_ref, wave_ref, power_ref):
    j = pl.program_id(0)
    pat = probe_ref.shape[1]
    width = ext_ref.shape[2]
    live = j < cnt[0]

    @pl.when(live)
    def _():
        r = roff[j]
        base = pl.multiple_of((r // 8) * 8, 8)
        span = pat + 8
        down = (span - (r - base)) % span
        shift = (width - coff[j]) % width

        def window(k):
            rows = pltpu.roll(ext_ref[k, pl.ds(base, span), :], down, 0)[:pat]
            return pltpu.roll(rows, shift, 1)[:, :pat]

        obj_re = window(0)
        obj_im = window(1)
        p_re = probe_ref[0]
        p_im = probe_ref[1]
        e_re = (p_re * obj_re - p_im * obj_im).astype(jnp.bfloat16)
        e_im = (p_re * obj_im + p_im * obj_re).astype(jnp.bfloat16)
        fr = fr_ref[...]
        fi = fi_ref[...]
        h_re = (_dot(fr, e_re) - _dot(fi, e_im)).astype(jnp.bfloat16)
        h_im = (_dot(fr, e_im) + _dot(fi, e_re)).astype(jnp.bfloat16)
        v_re = _dot(h_re, fr) - _dot(h_im, fi)
        v_im = _dot(h_re, fi) + _dot(h_im, fr)
        exit_ref[0, 0] = e_re
        exit_ref[0, 1] = e_im
        wave_ref[0, 0] = v_re
        wave_ref[0, 1] = v_im
        power_ref[0] = v_re * v_re + v_im * v_im

    @pl.when(jnp.logical_not(live))
    def _():
        power_ref[...] = jnp.zeros(power_ref.shape, jnp.float32)


def backward_kernel(roff, coff, cnt, exit_ref, wave_ref, model_ref, meas_ref, probe_ref, ppt_ref,
                    fr_ref, fi_ref, numer_ref, illum_ref):
    j = pl.program_id(0)
    pat = probe_ref.shape[1]
    width = numer_ref.shape[2]

    @pl.when(j == 0)
    def _():
        numer_ref[...] = jnp.zeros(numer_ref.shape, jnp.float32)
        illum_ref[...] = jnp.zeros(illum_ref.shape, jnp.float32)

    @pl.when(j < cnt[0])
    def _():
        r = roff[j]
        c = coff[j]
        base = pl.multiple_of((r // 8) * 8, 8)
        span = pat + 8
        v_re = wave_ref[0, 0]
        v_im = wave_ref[0, 1]
        scaling = jnp.sqrt(meas_ref[0]) / jnp.maximum(jnp.sqrt(model_ref[0]), 1.0)
        x_re = (scaling * v_re).astype(jnp.bfloat16)
        x_im = (scaling * v_im).astype(jnp.bfloat16)
        fr = fr_ref[...]
        fi = fi_ref[...]
        b_re = (_dot(fr, x_re) + _dot(fi, x_im)).astype(jnp.bfloat16)
        b_im = (_dot(fr, x_im) - _dot(fi, x_re)).astype(jnp.bfloat16)
        d_re = _dot(b_re, fr) + _dot(b_im, fi) - exit_ref[0, 0].astype(jnp.float32)
        d_im = _dot(b_im, fr) - _dot(b_re, fi) - exit_ref[0, 1].astype(jnp.float32)
        p_re = probe_ref[0]
        p_im = probe_ref[1]
        n_re = p_re * d_re + p_im * d_im
        n_im = p_re * d_im - p_im * d_re
        pad = jnp.zeros((pat, width - pat), jnp.float32)
        pad_rows = jnp.zeros((span - pat, width), jnp.float32)

        def place(a):
            wide = pltpu.roll(jnp.concatenate([a, pad], axis=1), c, 1)
            return pltpu.roll(jnp.concatenate([wide, pad_rows], axis=0), r - base, 0)

        numer_ref[0, pl.ds(base, span), :] += place(n_re)
        numer_ref[1, pl.ds(base, span), :] += place(n_im)
        illum_ref[pl.ds(base, span), :] += place(ppt_ref[...])


def run_forward(ext, probe2, fr, fi, roff, coff, cnt):
    slots = roff.shape[0]
    pat = probe2.shape[1]
    whole3 = lambda j, *_: (0, 0, 0)
    whole2 = lambda j, *_: (0, 0)
    per4 = lambda j, *_: (j, 0, 0, 0)
    per3 = lambda j, *_: (j, 0, 0)
    flops = slots * 8 * 2 * pat ** 3
    return pl.pallas_call(
        forward_kernel,
        grid_spec=pltpu.PrefetchScalarGridSpec(
            num_scalar_prefetch=3,
            grid=(slots,),
            in_specs=[
                pl.BlockSpec(ext.shape, whole3),
                pl.BlockSpec(probe2.shape, whole3),
                pl.BlockSpec(fr.shape, whole2),
                pl.BlockSpec(fi.shape, whole2),
            ],
            out_specs=[
                pl.BlockSpec((1, 2, pat, pat), per4),
                pl.BlockSpec((1, 2, pat, pat), per4),
                pl.BlockSpec((1, pat, pat), per3),
            ],
        ),
        out_shape=[
            jax.ShapeDtypeStruct((slots, 2, pat, pat), jnp.bfloat16),
            jax.ShapeDtypeStruct((slots, 2, pat, pat), jnp.float32),
            jax.ShapeDtypeStruct((slots, pat, pat), jnp.float32),
        ],
        compiler_params=pltpu.CompilerParams(dimension_semantics=("arbitrary",)),
        cost_estimate=pl.CostEstimate(flops=flops, transcendentals=0, bytes_accessed=8 * 1024 * 1024),
    )(roff, coff, cnt, ext, probe2, fr, fi)


def run_backward(exits, waves, model, measured, probe2, ppt, fr, fi, roff, coff, cnt, ext_rows, width):
    slots = roff.shape[0]
    pat = probe2.shape[1]
    whole3 = lambda j, *_: (0, 0, 0)
    whole2 = lambda j, *_: (0, 0)
    per4 = lambda j, *_: (j, 0, 0, 0)
    per3 = lambda j, *_: (j, 0, 0)
    flops = slots * 8 * 2 * pat ** 3
    return pl.pallas_call(
        backward_kernel,
        grid_spec=pltpu.PrefetchScalarGridSpec(
            num_scalar_prefetch=3,
            grid=(slots,),
            in_specs=[
                pl.BlockSpec((1, 2, pat, pat), per4),
                pl.BlockSpec((1, 2, pat, pat), per4),
                pl.BlockSpec((1, pat, pat), per3),
                pl.BlockSpec((1, pat, pat), per3),
                pl.BlockSpec(probe2.shape, whole3),
                pl.BlockSpec(ppt.shape, whole2),
                pl.BlockSpec(fr.shape, whole2),
                pl.BlockSpec(fi.shape, whole2),
            ],
            out_specs=[
                pl.BlockSpec((2, ext_rows, width), whole3),
                pl.BlockSpec((ext_rows, width), whole2),
            ],
        ),
        out_shape=[
            jax.ShapeDtypeStruct((2, ext_rows, width), jnp.float32),
            jax.ShapeDtypeStruct((ext_rows, width), jnp.float32),
        ],
        compiler_params=pltpu.CompilerParams(dimension_semantics=("arbitrary",)),
        cost_estimate=pl.CostEstimate(flops=flops, transcendentals=0, bytes_accessed=12 * 1024 * 1024),
    )(roff, coff, cnt, exits, waves, model, measured, probe2, ppt, fr, fi)


def local(object_field, probe, measured, row_offsets, col_offsets, tile_counts):
    rows_tile = object_field.shape[1]
    width = object_field.shape[2]
    pos_count = lax.axis_size("pos")
    mode_count = lax.axis_size("mode")
    my_mode = lax.axis_index("mode")
    share_rows = rows_tile // mode_count
    pattern = probe.shape[2]
    fr, fi = dft_tables(pattern)
    probe2 = probe[:, 0]

    probe_power = allreduce_mode(probe2[0] * probe2[0] + probe2[1] * probe2[1])

    before = lax.ppermute(object_field, "pos", neighbour_pairs(pos_count, 1))
    after = lax.ppermute(object_field, "pos", neighbour_pairs(pos_count, -1))
    ext = jnp.concatenate([before, object_field, after], axis=1)
    ext_rows = ext.shape[1]

    roff = row_offsets.astype(jnp.int32)
    coff = col_offsets.astype(jnp.int32)
    cnt = tile_counts.astype(jnp.int32)

    exits, waves, power = run_forward(ext, probe2, fr, fi, roff, coff, cnt)
    model = allreduce_mode(power)
    numer, illum = run_backward(
        exits, waves, model, measured, probe2, probe_power, fr, fi, roff, coff, cnt, ext_rows, width
    )

    top = numer[:, :rows_tile]
    mid = numer[:, rows_tile : 2 * rows_tile]
    bottom = numer[:, 2 * rows_tile :]
    tile_numer = (
        mid
        + lax.ppermute(bottom, "pos", neighbour_pairs(pos_count, 1))
        + lax.ppermute(top, "pos", neighbour_pairs(pos_count, -1))
    )
    numer_rows = reduce_scatter_mode(tile_numer)

    start = my_mode * share_rows
    illum_top = lax.dynamic_slice_in_dim(illum, start, share_rows, 0)
    illum_mid = lax.dynamic_slice_in_dim(illum, rows_tile + start, share_rows, 0)
    illum_bottom = lax.dynamic_slice_in_dim(illum, 2 * rows_tile + start, share_rows, 0)
    illum_rows = (
        illum_mid
        + lax.ppermute(illum_bottom, "pos", neighbour_pairs(pos_count, 1))
        + lax.ppermute(illum_top, "pos", neighbour_pairs(pos_count, -1))
    )

    own_rows = lax.dynamic_slice_in_dim(object_field, start, share_rows, 1)
    return own_rows + numer_rows / (illum_rows + 1.0)


def solution(mesh):
    in_specs = (
        P(None, "pos", None),
        P(None, "mode", None, None),
        P("pos", None, None),
        P("pos"),
        P("pos"),
        P("pos"),
    )
    out_specs = P(None, ("pos", "mode"), None)
    return jax.shard_map(local, mesh=mesh, in_specs=in_specs, out_specs=out_specs, check_vma=False)
```

```python
import math

import jax
import jax.numpy as jnp
from jax import lax
from jax.experimental import pallas as pl
from jax.experimental.pallas import tpu as pltpu
from jax.sharding import PartitionSpec as P


def dft_tables(pattern):
    counter = jnp.arange(pattern, dtype=jnp.int32)
    phases = counter[:, None] * counter[None, :] % pattern
    angles = phases.astype(jnp.float32) * (2.0 * math.pi / pattern)
    factor = 1.0 / math.sqrt(pattern)
    return (
        (jnp.cos(angles) * factor).astype(jnp.bfloat16),
        (-jnp.sin(angles) * factor).astype(jnp.bfloat16),
    )


def neighbour_pairs(size, step):
    if step > 0:
        return [(i, i + 1) for i in range(size - 1)]
    return [(i + 1, i) for i in range(size - 1)]


def mode_pairs():
    n = lax.axis_size("mode")
    chips = n // 2
    core = [(i, i ^ 1) for i in range(n)]
    near = [(i, i ^ 2) for i in range(n)]
    far = [(i, 2 * (chips - 1 - i // 2) + i % 2) for i in range(n)]
    return core, near, far


def allreduce_mode(x):
    core_pairs, near, far = mode_pairs()
    core = lax.axis_index("mode") % 2
    parts = x.reshape(2, 2, -1, x.shape[-1])
    keep = lax.dynamic_index_in_dim(parts, core, 0, keepdims=False)
    send = lax.dynamic_index_in_dim(parts, 1 - core, 0, keepdims=False)
    half = keep + lax.ppermute(send, "mode", core_pairs)
    qa, qb = half[0], half[1]
    qa = qa + lax.ppermute(qa, "mode", near)
    qb = qb + lax.ppermute(qb, "mode", far)
    qa = qa + lax.ppermute(qa, "mode", far)
    qb = qb + lax.ppermute(qb, "mode", near)
    half = jnp.stack([qa, qb])
    other = lax.ppermute(half, "mode", core_pairs)
    first = jnp.where(core == 0, half, other)
    second = jnp.where(core == 0, other, half)
    return jnp.stack([first, second]).reshape(x.shape)


def reduce_scatter_mode(x):
    core_pairs, near, far = mode_pairs()
    n = lax.axis_size("mode")
    m = lax.axis_index("mode")
    c, rows, w = x.shape
    x = x.reshape(c, 2, 2, 2, rows // n, w)
    for pairs, dim, d in ((core_pairs, 3, 1), (far, 1, 4), (near, 1, 2)):
        bit = (m // d) % 2
        keep = lax.dynamic_index_in_dim(x, bit, axis=dim, keepdims=False)
        send = lax.dynamic_index_in_dim(x, 1 - bit, axis=dim, keepdims=False)
        x = keep + lax.ppermute(send, "mode", pairs)
    return x.reshape(c, rows // n, w)


def _dot(a, b):
    return jnp.dot(a, b, preferred_element_type=jnp.float32)


def forward_kernel(roff, coff, cnt, ext_ref, probe_ref, fr_ref, fi_ref, ppt_ref, exit_ref, wave_ref, power_ref):
    j = pl.program_id(0)
    pat = probe_ref.shape[1]
    width = ext_ref.shape[2]
    live = j < cnt[0]

    @pl.when(live)
    def _():
        r = roff[j]
        base = pl.multiple_of((r // 8) * 8, 8)
        span = pat + 8
        down = (span - (r - base)) % span
        shift = (width - coff[j]) % width

        def window(k):
            rows = pltpu.roll(ext_ref[k, pl.ds(base, span), :], down, 0)[:pat]
            return pltpu.roll(rows, shift, 1)[:, :pat]

        obj_re = window(0)
        obj_im = window(1)
        p_re = probe_ref[0]
        p_im = probe_ref[1]
        e_re = (p_re * obj_re - p_im * obj_im).astype(jnp.bfloat16)
        e_im = (p_re * obj_im + p_im * obj_re).astype(jnp.bfloat16)
        fr = fr_ref[...]
        fi = fi_ref[...]
        h_re = (_dot(fr, e_re) - _dot(fi, e_im)).astype(jnp.bfloat16)
        h_im = (_dot(fr, e_im) + _dot(fi, e_re)).astype(jnp.bfloat16)
        v_re = _dot(h_re, fr) - _dot(h_im, fi)
        v_im = _dot(h_re, fi) + _dot(h_im, fr)
        exit_ref[0, 0] = e_re
        exit_ref[0, 1] = e_im
        wave_ref[0, 0] = v_re
        wave_ref[0, 1] = v_im
        power_ref[0] = v_re * v_re + v_im * v_im

    @pl.when(jnp.logical_not(live))
    def _():
        power_ref[...] = jnp.zeros(power_ref.shape, jnp.float32)


def backward_kernel(roff, coff, cnt, exit_ref, wave_ref, model_ref, meas_ref, probe_ref, ppt_ref,
                    fr_ref, fi_ref, numer_ref, illum_ref):
    j = pl.program_id(0)
    pat = probe_ref.shape[1]
    width = numer_ref.shape[2]

    @pl.when(j == 0)
    def _():
        numer_ref[...] = jnp.zeros(numer_ref.shape, jnp.float32)
        illum_ref[...] = jnp.zeros(illum_ref.shape, jnp.float32)

    @pl.when(j < cnt[0])
    def _():
        r = roff[j]
        c = coff[j]
        base = pl.multiple_of((r // 8) * 8, 8)
        span = pat + 8
        v_re = wave_ref[0, 0]
        v_im = wave_ref[0, 1]
        scaling = jnp.sqrt(meas_ref[0]) / jnp.maximum(jnp.sqrt(model_ref[0]), 1.0)
        x_re = (scaling * v_re).astype(jnp.bfloat16)
        x_im = (scaling * v_im).astype(jnp.bfloat16)
        fr = fr_ref[...]
        fi = fi_ref[...]
        b_re = (_dot(fr, x_re) + _dot(fi, x_im)).astype(jnp.bfloat16)
        b_im = (_dot(fr, x_im) - _dot(fi, x_re)).astype(jnp.bfloat16)
        d_re = _dot(b_re, fr) + _dot(b_im, fi) - exit_ref[0, 0].astype(jnp.float32)
        d_im = _dot(b_im, fr) - _dot(b_re, fi) - exit_ref[0, 1].astype(jnp.float32)
        p_re = probe_ref[0]
        p_im = probe_ref[1]
        n_re = p_re * d_re + p_im * d_im
        n_im = p_re * d_im - p_im * d_re
        pad = jnp.zeros((pat, width - pat), jnp.float32)
        pad_rows = jnp.zeros((span - pat, width), jnp.float32)

        def place(a):
            wide = pltpu.roll(jnp.concatenate([a, pad], axis=1), c, 1)
            return pltpu.roll(jnp.concatenate([wide, pad_rows], axis=0), r - base, 0)

        numer_ref[0, pl.ds(base, span), :] += place(n_re)
        numer_ref[1, pl.ds(base, span), :] += place(n_im)
        illum_ref[pl.ds(base, span), :] += place(ppt_ref[...])


def run_forward(ext, probe2, fr, fi, ppt, roff, coff, cnt):
    slots = roff.shape[0]
    pat = probe2.shape[1]
    whole3 = lambda j, *_: (0, 0, 0)
    whole2 = lambda j, *_: (0, 0)
    per4 = lambda j, *_: (j, 0, 0, 0)
    per3 = lambda j, *_: (j, 0, 0)
    flops = slots * 8 * 2 * pat ** 3
    return pl.pallas_call(
        forward_kernel,
        grid_spec=pltpu.PrefetchScalarGridSpec(
            num_scalar_prefetch=3,
            grid=(slots,),
            in_specs=[
                pl.BlockSpec(ext.shape, whole3),
                pl.BlockSpec(probe2.shape, whole3),
                pl.BlockSpec(fr.shape, whole2),
                pl.BlockSpec(fi.shape, whole2),
                pl.BlockSpec(ppt.shape, whole2),
            ],
            out_specs=[
                pl.BlockSpec((1, 2, pat, pat), per4),
                pl.BlockSpec((1, 2, pat, pat), per4),
                pl.BlockSpec((1, pat, pat), per3),
            ],
        ),
        out_shape=[
            jax.ShapeDtypeStruct((slots, 2, pat, pat), jnp.bfloat16),
            jax.ShapeDtypeStruct((slots, 2, pat, pat), jnp.float32),
            jax.ShapeDtypeStruct((slots, pat, pat), jnp.float32),
        ],
        compiler_params=pltpu.CompilerParams(dimension_semantics=("arbitrary",)),
        cost_estimate=pl.CostEstimate(flops=flops, transcendentals=0, bytes_accessed=8 * 1024 * 1024),
    )(roff, coff, cnt, ext, probe2, fr, fi, ppt)


def run_backward(exits, waves, model, measured, probe2, ppt, fr, fi, roff, coff, cnt, ext_rows, width):
    slots = roff.shape[0]
    pat = probe2.shape[1]
    whole3 = lambda j, *_: (0, 0, 0)
    whole2 = lambda j, *_: (0, 0)
    per4 = lambda j, *_: (j, 0, 0, 0)
    per3 = lambda j, *_: (j, 0, 0)
    flops = slots * 8 * 2 * pat ** 3
    return pl.pallas_call(
        backward_kernel,
        grid_spec=pltpu.PrefetchScalarGridSpec(
            num_scalar_prefetch=3,
            grid=(slots,),
            in_specs=[
                pl.BlockSpec((1, 2, pat, pat), per4),
                pl.BlockSpec((1, 2, pat, pat), per4),
                pl.BlockSpec((1, pat, pat), per3),
                pl.BlockSpec((1, pat, pat), per3),
                pl.BlockSpec(probe2.shape, whole3),
                pl.BlockSpec(ppt.shape, whole2),
                pl.BlockSpec(fr.shape, whole2),
                pl.BlockSpec(fi.shape, whole2),
            ],
            out_specs=[
                pl.BlockSpec((2, ext_rows, width), whole3),
                pl.BlockSpec((ext_rows, width), whole2),
            ],
        ),
        out_shape=[
            jax.ShapeDtypeStruct((2, ext_rows, width), jnp.float32),
            jax.ShapeDtypeStruct((ext_rows, width), jnp.float32),
        ],
        compiler_params=pltpu.CompilerParams(dimension_semantics=("arbitrary",)),
        cost_estimate=pl.CostEstimate(flops=flops, transcendentals=0, bytes_accessed=12 * 1024 * 1024),
    )(roff, coff, cnt, exits, waves, model, measured, probe2, ppt, fr, fi)


def local(object_field, probe, measured, row_offsets, col_offsets, tile_counts):
    rows_tile = object_field.shape[1]
    width = object_field.shape[2]
    pos_count = lax.axis_size("pos")
    mode_count = lax.axis_size("mode")
    my_mode = lax.axis_index("mode")
    share_rows = rows_tile // mode_count
    pattern = probe.shape[2]
    fr, fi = dft_tables(pattern)
    probe2 = probe[:, 0]

    probe_power = allreduce_mode(probe2[0] * probe2[0] + probe2[1] * probe2[1])

    before = lax.ppermute(object_field, "pos", neighbour_pairs(pos_count, 1))
    after = lax.ppermute(object_field, "pos", neighbour_pairs(pos_count, -1))
    ext = jnp.concatenate([before, object_field, after], axis=1)
    ext_rows = ext.shape[1]

    roff = row_offsets.astype(jnp.int32)
    coff = col_offsets.astype(jnp.int32)
    cnt = tile_counts.astype(jnp.int32)

    exits, waves, power = run_forward(ext, probe2, fr, fi, probe_power, roff, coff, cnt)
    model = allreduce_mode(power)
    numer, illum = run_backward(
        exits, waves, model, measured, probe2, probe_power, fr, fi, roff, coff, cnt, ext_rows, width
    )

    top = numer[:, :rows_tile]
    mid = numer[:, rows_tile : 2 * rows_tile]
    bottom = numer[:, 2 * rows_tile :]
    tile_numer = (
        mid
        + lax.ppermute(bottom, "pos", neighbour_pairs(pos_count, 1))
        + lax.ppermute(top, "pos", neighbour_pairs(pos_count, -1))
    )
    numer_rows = reduce_scatter_mode(tile_numer)

    start = my_mode * share_rows
    illum_top = lax.dynamic_slice_in_dim(illum, start, share_rows, 0)
    illum_mid = lax.dynamic_slice_in_dim(illum, rows_tile + start, share_rows, 0)
    illum_bottom = lax.dynamic_slice_in_dim(illum, 2 * rows_tile + start, share_rows, 0)
    illum_rows = (
        illum_mid
        + lax.ppermute(illum_bottom, "pos", neighbour_pairs(pos_count, 1))
        + lax.ppermute(illum_top, "pos", neighbour_pairs(pos_count, -1))
    )

    own_rows = lax.dynamic_slice_in_dim(object_field, start, share_rows, 1)
    return own_rows + numer_rows / (illum_rows + 1.0)


def solution(mesh):
    in_specs = (
        P(None, "pos", None),
        P(None, "mode", None, None),
        P("pos", None, None),
        P("pos"),
        P("pos"),
        P("pos"),
    )
    out_specs = P(None, ("pos", "mode"), None)
    return jax.shard_map(local, mesh=mesh, in_specs=in_specs, out_specs=out_specs, check_vma=False)
```

```python
import math

import jax
import jax.numpy as jnp
from jax import lax
from jax.experimental import pallas as pl
from jax.experimental.pallas import tpu as pltpu
from jax.sharding import PartitionSpec as P


def dft_tables(pattern):
    counter = jnp.arange(pattern, dtype=jnp.int32)
    phases = counter[:, None] * counter[None, :] % pattern
    angles = phases.astype(jnp.float32) * (2.0 * math.pi / pattern)
    factor = 1.0 / math.sqrt(pattern)
    return (
        (jnp.cos(angles) * factor).astype(jnp.bfloat16),
        (-jnp.sin(angles) * factor).astype(jnp.bfloat16),
    )


def neighbour_pairs(size, step):
    if step > 0:
        return [(i, i + 1) for i in range(size - 1)]
    return [(i + 1, i) for i in range(size - 1)]


def mode_pairs():
    n = lax.axis_size("mode")
    chips = n // 2
    core = [(i, i ^ 1) for i in range(n)]
    near = [(i, i ^ 2) for i in range(n)]
    far = [(i, 2 * (chips - 1 - i // 2) + i % 2) for i in range(n)]
    return core, near, far


def allreduce_mode(x):
    core_pairs, near, far = mode_pairs()
    core = lax.axis_index("mode") % 2
    parts = x.reshape(2, 2, -1, x.shape[-1])
    keep = lax.dynamic_index_in_dim(parts, core, 0, keepdims=False)
    send = lax.dynamic_index_in_dim(parts, 1 - core, 0, keepdims=False)
    half = keep + lax.ppermute(send, "mode", core_pairs)
    qa, qb = half[0], half[1]
    qa = qa + lax.ppermute(qa, "mode", near)
    qb = qb + lax.ppermute(qb, "mode", far)
    qa = qa + lax.ppermute(qa, "mode", far)
    qb = qb + lax.ppermute(qb, "mode", near)
    half = jnp.stack([qa, qb])
    other = lax.ppermute(half, "mode", core_pairs)
    first = jnp.where(core == 0, half, other)
    second = jnp.where(core == 0, other, half)
    return jnp.stack([first, second]).reshape(x.shape)


def reduce_scatter_mode(x):
    core_pairs, near, far = mode_pairs()
    n = lax.axis_size("mode")
    m = lax.axis_index("mode")
    c, rows, w = x.shape
    x = x.reshape(c, 2, 2, 2, rows // n, w)
    for pairs, dim, d in ((core_pairs, 3, 1), (far, 1, 4), (near, 1, 2)):
        bit = (m // d) % 2
        keep = lax.dynamic_index_in_dim(x, bit, axis=dim, keepdims=False)
        send = lax.dynamic_index_in_dim(x, 1 - bit, axis=dim, keepdims=False)
        x = keep + lax.ppermute(send, "mode", pairs)
    return x.reshape(c, rows // n, w)


def _dot(a, b):
    return jnp.dot(a, b, preferred_element_type=jnp.float32)


def forward_kernel(roff, coff, cnt, before_ref, own_ref, after_ref, probe_ref, fr_ref, fi_ref,
                   exit_ref, wave_ref, power_ref, ext_ref):
    j = pl.program_id(0)
    pat = probe_ref.shape[1]
    width = ext_ref.shape[2]
    band = own_ref.shape[1]
    live = j < cnt[0]

    @pl.when(j == 0)
    def _():
        ext_ref[:, :band, :] = before_ref[...]
        ext_ref[:, band : 2 * band, :] = own_ref[...]
        ext_ref[:, 2 * band :, :] = after_ref[...]
        p_re = probe_ref[0]
        p_im = probe_ref[1]
        power_ref[power_ref.shape[0] - 1] = p_re * p_re + p_im * p_im

    @pl.when(live)
    def _():
        r = roff[j]
        base = pl.multiple_of((r // 8) * 8, 8)
        span = pat + 8
        down = (span - (r - base)) % span
        shift = (width - coff[j]) % width

        def window(k):
            rows = pltpu.roll(ext_ref[k, pl.ds(base, span), :], down, 0)[:pat]
            return pltpu.roll(rows, shift, 1)[:, :pat]

        obj_re = window(0)
        obj_im = window(1)
        p_re = probe_ref[0]
        p_im = probe_ref[1]
        e_re = (p_re * obj_re - p_im * obj_im).astype(jnp.bfloat16)
        e_im = (p_re * obj_im + p_im * obj_re).astype(jnp.bfloat16)
        fr = fr_ref[...]
        fi = fi_ref[...]
        h_re = (_dot(fr, e_re) - _dot(fi, e_im)).astype(jnp.bfloat16)
        h_im = (_dot(fr, e_im) + _dot(fi, e_re)).astype(jnp.bfloat16)
        v_re = _dot(h_re, fr) - _dot(h_im, fi)
        v_im = _dot(h_re, fi) + _dot(h_im, fr)
        exit_ref[0, 0] = e_re
        exit_ref[0, 1] = e_im
        wave_ref[0, 0] = v_re
        wave_ref[0, 1] = v_im
        power_ref[j] = v_re * v_re + v_im * v_im

    @pl.when(jnp.logical_not(live))
    def _():
        power_ref[j] = jnp.zeros((pat, pat), jnp.float32)


def backward_kernel(roff, coff, cnt, exit_ref, wave_ref, model_ref, meas_ref, probe_ref, ppt_ref,
                    fr_ref, fi_ref, numer_ref, illum_ref):
    j = pl.program_id(0)
    pat = probe_ref.shape[1]
    width = numer_ref.shape[2]

    @pl.when(j == 0)
    def _():
        numer_ref[...] = jnp.zeros(numer_ref.shape, jnp.float32)
        illum_ref[...] = jnp.zeros(illum_ref.shape, jnp.float32)

    @pl.when(j < cnt[0])
    def _():
        r = roff[j]
        c = coff[j]
        base = pl.multiple_of((r // 8) * 8, 8)
        span = pat + 8
        v_re = wave_ref[0, 0]
        v_im = wave_ref[0, 1]
        scaling = jnp.sqrt(meas_ref[0]) / jnp.maximum(jnp.sqrt(model_ref[0]), 1.0)
        x_re = (scaling * v_re).astype(jnp.bfloat16)
        x_im = (scaling * v_im).astype(jnp.bfloat16)
        fr = fr_ref[...]
        fi = fi_ref[...]
        b_re = (_dot(fr, x_re) + _dot(fi, x_im)).astype(jnp.bfloat16)
        b_im = (_dot(fr, x_im) - _dot(fi, x_re)).astype(jnp.bfloat16)
        d_re = _dot(b_re, fr) + _dot(b_im, fi) - exit_ref[0, 0].astype(jnp.float32)
        d_im = _dot(b_im, fr) - _dot(b_re, fi) - exit_ref[0, 1].astype(jnp.float32)
        p_re = probe_ref[0]
        p_im = probe_ref[1]
        n_re = p_re * d_re + p_im * d_im
        n_im = p_re * d_im - p_im * d_re
        pad = jnp.zeros((pat, width - pat), jnp.float32)
        pad_rows = jnp.zeros((span - pat, width), jnp.float32)

        def place(a):
            wide = pltpu.roll(jnp.concatenate([a, pad], axis=1), c, 1)
            return pltpu.roll(jnp.concatenate([wide, pad_rows], axis=0), r - base, 0)

        numer_ref[0, pl.ds(base, span), :] += place(n_re)
        numer_ref[1, pl.ds(base, span), :] += place(n_im)
        illum_ref[pl.ds(base, span), :] += place(ppt_ref[0])


def run_forward(before, own, after, probe2, fr, fi, roff, coff, cnt):
    slots = roff.shape[0]
    pat = probe2.shape[1]
    whole3 = lambda j, *_: (0, 0, 0)
    whole2 = lambda j, *_: (0, 0)
    per4 = lambda j, *_: (j, 0, 0, 0)
    flops = slots * 8 * 2 * pat ** 3
    ext_shape = (2, 3 * own.shape[1], own.shape[2])
    return pl.pallas_call(
        forward_kernel,
        grid_spec=pltpu.PrefetchScalarGridSpec(
            num_scalar_prefetch=3,
            grid=(slots,),
            in_specs=[
                pl.BlockSpec(before.shape, whole3),
                pl.BlockSpec(own.shape, whole3),
                pl.BlockSpec(after.shape, whole3),
                pl.BlockSpec(probe2.shape, whole3),
                pl.BlockSpec(fr.shape, whole2),
                pl.BlockSpec(fi.shape, whole2),
            ],
            out_specs=[
                pl.BlockSpec((1, 2, pat, pat), per4),
                pl.BlockSpec((1, 2, pat, pat), per4),
                pl.BlockSpec((slots + 1, pat, pat), whole3),
            ],
            scratch_shapes=[pltpu.VMEM(ext_shape, jnp.float32)],
        ),
        out_shape=[
            jax.ShapeDtypeStruct((slots, 2, pat, pat), jnp.bfloat16),
            jax.ShapeDtypeStruct((slots, 2, pat, pat), jnp.float32),
            jax.ShapeDtypeStruct((slots + 1, pat, pat), jnp.float32),
        ],
        compiler_params=pltpu.CompilerParams(dimension_semantics=("arbitrary",)),
        cost_estimate=pl.CostEstimate(flops=flops, transcendentals=0, bytes_accessed=8 * 1024 * 1024),
    )(roff, coff, cnt, before, own, after, probe2, fr, fi)


def run_backward(exits, waves, totals, measured, probe2, fr, fi, roff, coff, cnt, ext_rows, width):
    slots = roff.shape[0]
    pat = probe2.shape[1]
    whole3 = lambda j, *_: (0, 0, 0)
    whole2 = lambda j, *_: (0, 0)
    per4 = lambda j, *_: (j, 0, 0, 0)
    per3 = lambda j, *_: (j, 0, 0)
    flops = slots * 8 * 2 * pat ** 3
    return pl.pallas_call(
        backward_kernel,
        grid_spec=pltpu.PrefetchScalarGridSpec(
            num_scalar_prefetch=3,
            grid=(slots,),
            in_specs=[
                pl.BlockSpec((1, 2, pat, pat), per4),
                pl.BlockSpec((1, 2, pat, pat), per4),
                pl.BlockSpec((1, pat, pat), per3),
                pl.BlockSpec((1, pat, pat), per3),
                pl.BlockSpec(probe2.shape, whole3),
                pl.BlockSpec((1, pat, pat), lambda j, *_: (slots, 0, 0)),
                pl.BlockSpec(fr.shape, whole2),
                pl.BlockSpec(fi.shape, whole2),
            ],
            out_specs=[
                pl.BlockSpec((2, ext_rows, width), whole3),
                pl.BlockSpec((ext_rows, width), whole2),
            ],
        ),
        out_shape=[
            jax.ShapeDtypeStruct((2, ext_rows, width), jnp.float32),
            jax.ShapeDtypeStruct((ext_rows, width), jnp.float32),
        ],
        compiler_params=pltpu.CompilerParams(dimension_semantics=("arbitrary",)),
        cost_estimate=pl.CostEstimate(flops=flops, transcendentals=0, bytes_accessed=12 * 1024 * 1024),
    )(roff, coff, cnt, exits, waves, totals, measured, probe2, totals, fr, fi)


def local(object_field, probe, measured, row_offsets, col_offsets, tile_counts):
    rows_tile = object_field.shape[1]
    width = object_field.shape[2]
    pos_count = lax.axis_size("pos")
    mode_count = lax.axis_size("mode")
    my_mode = lax.axis_index("mode")
    share_rows = rows_tile // mode_count
    pattern = probe.shape[2]
    fr, fi = dft_tables(pattern)
    probe2 = probe[:, 0]

    before = lax.ppermute(object_field, "pos", neighbour_pairs(pos_count, 1))
    after = lax.ppermute(object_field, "pos", neighbour_pairs(pos_count, -1))
    ext_rows = 3 * rows_tile

    roff = row_offsets.astype(jnp.int32)
    coff = col_offsets.astype(jnp.int32)
    cnt = tile_counts.astype(jnp.int32)

    exits, waves, power = run_forward(before, object_field, after, probe2, fr, fi, roff, coff, cnt)
    totals = allreduce_mode(power)
    numer, illum = run_backward(
        exits, waves, totals, measured, probe2, fr, fi, roff, coff, cnt, ext_rows, width
    )

    core_pairs, near, far = mode_pairs()
    core = my_mode % 2
    blocks = numer.reshape(2, 3, 2, 2, 2, share_rows, width)
    keep = lax.dynamic_index_in_dim(blocks, core, axis=4, keepdims=False)
    send = lax.dynamic_index_in_dim(blocks, 1 - core, axis=4, keepdims=False)
    blocks = keep + lax.ppermute(send, "mode", core_pairs)
    band_rows = 2 * 4 * share_rows
    own_illum = lax.dynamic_index_in_dim(
        illum.reshape(3, mode_count, share_rows, width), my_mode, axis=1, keepdims=False
    )
    to_next = jnp.concatenate([blocks[:, 2].reshape(band_rows, width), own_illum[2]], axis=0)
    to_prev = jnp.concatenate([blocks[:, 0].reshape(band_rows, width), own_illum[0]], axis=0)
    from_prev = lax.ppermute(to_next, "pos", neighbour_pairs(pos_count, 1))
    from_next = lax.ppermute(to_prev, "pos", neighbour_pairs(pos_count, -1))
    tile = (
        blocks[:, 1]
        + from_prev[:band_rows].reshape(blocks[:, 1].shape)
        + from_next[:band_rows].reshape(blocks[:, 1].shape)
    )
    illum_rows = own_illum[1] + from_prev[band_rows:] + from_next[band_rows:]
    for pairs, d in ((far, 4), (near, 2)):
        bit = (my_mode // d) % 2
        keep = lax.dynamic_index_in_dim(tile, bit, axis=1, keepdims=False)
        send = lax.dynamic_index_in_dim(tile, 1 - bit, axis=1, keepdims=False)
        tile = keep + lax.ppermute(send, "mode", pairs)

    start = my_mode * share_rows
    own_rows = lax.dynamic_slice_in_dim(object_field, start, share_rows, 1)
    return own_rows + tile / (illum_rows + 1.0)


def solution(mesh):
    in_specs = (
        P(None, "pos", None),
        P(None, "mode", None, None),
        P("pos", None, None),
        P("pos"),
        P("pos"),
        P("pos"),
    )
    out_specs = P(None, ("pos", "mode"), None)
    return jax.shard_map(local, mesh=mesh, in_specs=in_specs, out_specs=out_specs, check_vma=False)
```

```python
import math

import jax
import jax.numpy as jnp
from jax import lax
from jax.experimental import pallas as pl
from jax.experimental.pallas import tpu as pltpu
from jax.sharding import PartitionSpec as P


def dft_tables(pattern):
    counter = jnp.arange(pattern, dtype=jnp.int32)
    phases = counter[:, None] * counter[None, :] % pattern
    angles = phases.astype(jnp.float32) * (2.0 * math.pi / pattern)
    factor = 1.0 / math.sqrt(pattern)
    return (
        (jnp.cos(angles) * factor).astype(jnp.bfloat16),
        (-jnp.sin(angles) * factor).astype(jnp.bfloat16),
    )


def neighbour_pairs(size, step):
    if step > 0:
        return [(i, i + 1) for i in range(size - 1)]
    return [(i + 1, i) for i in range(size - 1)]


def mode_pairs():
    n = lax.axis_size("mode")
    chips = n // 2
    core = [(i, i ^ 1) for i in range(n)]
    near = [(i, i ^ 2) for i in range(n)]
    far = [(i, 2 * (chips - 1 - i // 2) + i % 2) for i in range(n)]
    return core, near, far


def allreduce_mode(x):
    n = lax.axis_size("mode")
    chunks = x.reshape(n, -1, x.shape[-1])
    mine = jnp.sum(lax.all_to_all(chunks, "mode", 0, 0), axis=0)
    spread = jnp.broadcast_to(mine[None], chunks.shape)
    return lax.all_to_all(spread, "mode", 0, 0).reshape(x.shape)


def reduce_scatter_mode(x):
    core_pairs, near, far = mode_pairs()
    n = lax.axis_size("mode")
    m = lax.axis_index("mode")
    c, rows, w = x.shape
    x = x.reshape(c, 2, 2, 2, rows // n, w)
    for pairs, dim, d in ((core_pairs, 3, 1), (far, 1, 4), (near, 1, 2)):
        bit = (m // d) % 2
        keep = lax.dynamic_index_in_dim(x, bit, axis=dim, keepdims=False)
        send = lax.dynamic_index_in_dim(x, 1 - bit, axis=dim, keepdims=False)
        x = keep + lax.ppermute(send, "mode", pairs)
    return x.reshape(c, rows // n, w)


def _dot(a, b):
    return jnp.dot(a, b, preferred_element_type=jnp.float32)


def forward_kernel(roff, coff, cnt, before_ref, own_ref, after_ref, probe_ref, fr_ref, fi_ref,
                   exit_ref, wave_ref, power_ref, ext_ref):
    j = pl.program_id(0)
    pat = probe_ref.shape[1]
    width = ext_ref.shape[2]
    band = own_ref.shape[1]
    live = j < cnt[0]

    @pl.when(j == 0)
    def _():
        ext_ref[:, :band, :] = before_ref[...]
        ext_ref[:, band : 2 * band, :] = own_ref[...]
        ext_ref[:, 2 * band :, :] = after_ref[...]
        p_re = probe_ref[0]
        p_im = probe_ref[1]
        power_ref[power_ref.shape[0] - 1] = p_re * p_re + p_im * p_im

    @pl.when(live)
    def _():
        r = roff[j]
        base = pl.multiple_of((r // 8) * 8, 8)
        span = pat + 8
        down = (span - (r - base)) % span
        shift = (width - coff[j]) % width

        def window(k):
            rows = pltpu.roll(ext_ref[k, pl.ds(base, span), :], down, 0)[:pat]
            return pltpu.roll(rows, shift, 1)[:, :pat]

        obj_re = window(0)
        obj_im = window(1)
        p_re = probe_ref[0]
        p_im = probe_ref[1]
        e_re = (p_re * obj_re - p_im * obj_im).astype(jnp.bfloat16)
        e_im = (p_re * obj_im + p_im * obj_re).astype(jnp.bfloat16)
        fr = fr_ref[...]
        fi = fi_ref[...]
        h_re = (_dot(fr, e_re) - _dot(fi, e_im)).astype(jnp.bfloat16)
        h_im = (_dot(fr, e_im) + _dot(fi, e_re)).astype(jnp.bfloat16)
        v_re = _dot(h_re, fr) - _dot(h_im, fi)
        v_im = _dot(h_re, fi) + _dot(h_im, fr)
        exit_ref[0, 0] = e_re
        exit_ref[0, 1] = e_im
        wave_ref[0, 0] = v_re
        wave_ref[0, 1] = v_im
        power_ref[j] = v_re * v_re + v_im * v_im

    @pl.when(jnp.logical_not(live))
    def _():
        power_ref[j] = jnp.zeros((pat, pat), jnp.float32)


def backward_kernel(roff, coff, cnt, exit_ref, wave_ref, model_ref, meas_ref, probe_ref, ppt_ref,
                    fr_ref, fi_ref, numer_ref, illum_ref):
    j = pl.program_id(0)
    pat = probe_ref.shape[1]
    width = numer_ref.shape[2]

    @pl.when(j == 0)
    def _():
        numer_ref[...] = jnp.zeros(numer_ref.shape, jnp.float32)
        illum_ref[...] = jnp.zeros(illum_ref.shape, jnp.float32)

    @pl.when(j < cnt[0])
    def _():
        r = roff[j]
        c = coff[j]
        base = pl.multiple_of((r // 8) * 8, 8)
        span = pat + 8
        v_re = wave_ref[0, 0]
        v_im = wave_ref[0, 1]
        scaling = jnp.sqrt(meas_ref[0]) / jnp.maximum(jnp.sqrt(model_ref[0]), 1.0)
        x_re = (scaling * v_re).astype(jnp.bfloat16)
        x_im = (scaling * v_im).astype(jnp.bfloat16)
        fr = fr_ref[...]
        fi = fi_ref[...]
        b_re = (_dot(fr, x_re) + _dot(fi, x_im)).astype(jnp.bfloat16)
        b_im = (_dot(fr, x_im) - _dot(fi, x_re)).astype(jnp.bfloat16)
        d_re = _dot(b_re, fr) + _dot(b_im, fi) - exit_ref[0, 0].astype(jnp.float32)
        d_im = _dot(b_im, fr) - _dot(b_re, fi) - exit_ref[0, 1].astype(jnp.float32)
        p_re = probe_ref[0]
        p_im = probe_ref[1]
        n_re = p_re * d_re + p_im * d_im
        n_im = p_re * d_im - p_im * d_re
        pad = jnp.zeros((pat, width - pat), jnp.float32)
        pad_rows = jnp.zeros((span - pat, width), jnp.float32)

        def place(a):
            wide = pltpu.roll(jnp.concatenate([a, pad], axis=1), c, 1)
            return pltpu.roll(jnp.concatenate([wide, pad_rows], axis=0), r - base, 0)

        numer_ref[0, pl.ds(base, span), :] += place(n_re)
        numer_ref[1, pl.ds(base, span), :] += place(n_im)
        illum_ref[pl.ds(base, span), :] += place(ppt_ref[0])


def run_forward(before, own, after, probe2, fr, fi, roff, coff, cnt):
    slots = roff.shape[0]
    pat = probe2.shape[1]
    whole3 = lambda j, *_: (0, 0, 0)
    whole2 = lambda j, *_: (0, 0)
    per4 = lambda j, *_: (j, 0, 0, 0)
    flops = slots * 8 * 2 * pat ** 3
    ext_shape = (2, 3 * own.shape[1], own.shape[2])
    return pl.pallas_call(
        forward_kernel,
        grid_spec=pltpu.PrefetchScalarGridSpec(
            num_scalar_prefetch=3,
            grid=(slots,),
            in_specs=[
                pl.BlockSpec(before.shape, whole3),
                pl.BlockSpec(own.shape, whole3),
                pl.BlockSpec(after.shape, whole3),
                pl.BlockSpec(probe2.shape, whole3),
                pl.BlockSpec(fr.shape, whole2),
                pl.BlockSpec(fi.shape, whole2),
            ],
            out_specs=[
                pl.BlockSpec((1, 2, pat, pat), per4),
                pl.BlockSpec((1, 2, pat, pat), per4),
                pl.BlockSpec((slots + 1, pat, pat), whole3),
            ],
            scratch_shapes=[pltpu.VMEM(ext_shape, jnp.float32)],
        ),
        out_shape=[
            jax.ShapeDtypeStruct((slots, 2, pat, pat), jnp.bfloat16),
            jax.ShapeDtypeStruct((slots, 2, pat, pat), jnp.float32),
            jax.ShapeDtypeStruct((slots + 1, pat, pat), jnp.float32),
        ],
        compiler_params=pltpu.CompilerParams(dimension_semantics=("arbitrary",)),
        cost_estimate=pl.CostEstimate(flops=flops, transcendentals=0, bytes_accessed=8 * 1024 * 1024),
    )(roff, coff, cnt, before, own, after, probe2, fr, fi)


def run_backward(exits, waves, totals, measured, probe2, fr, fi, roff, coff, cnt, ext_rows, width):
    slots = roff.shape[0]
    pat = probe2.shape[1]
    whole3 = lambda j, *_: (0, 0, 0)
    whole2 = lambda j, *_: (0, 0)
    per4 = lambda j, *_: (j, 0, 0, 0)
    per3 = lambda j, *_: (j, 0, 0)
    flops = slots * 8 * 2 * pat ** 3
    return pl.pallas_call(
        backward_kernel,
        grid_spec=pltpu.PrefetchScalarGridSpec(
            num_scalar_prefetch=3,
            grid=(slots,),
            in_specs=[
                pl.BlockSpec((1, 2, pat, pat), per4),
                pl.BlockSpec((1, 2, pat, pat), per4),
                pl.BlockSpec((1, pat, pat), per3),
                pl.BlockSpec((1, pat, pat), per3),
                pl.BlockSpec(probe2.shape, whole3),
                pl.BlockSpec((1, pat, pat), lambda j, *_: (slots, 0, 0)),
                pl.BlockSpec(fr.shape, whole2),
                pl.BlockSpec(fi.shape, whole2),
            ],
            out_specs=[
                pl.BlockSpec((2, ext_rows, width), whole3),
                pl.BlockSpec((ext_rows, width), whole2),
            ],
        ),
        out_shape=[
            jax.ShapeDtypeStruct((2, ext_rows, width), jnp.float32),
            jax.ShapeDtypeStruct((ext_rows, width), jnp.float32),
        ],
        compiler_params=pltpu.CompilerParams(dimension_semantics=("arbitrary",)),
        cost_estimate=pl.CostEstimate(flops=flops, transcendentals=0, bytes_accessed=12 * 1024 * 1024),
    )(roff, coff, cnt, exits, waves, totals, measured, probe2, totals, fr, fi)


def local(object_field, probe, measured, row_offsets, col_offsets, tile_counts):
    rows_tile = object_field.shape[1]
    width = object_field.shape[2]
    pos_count = lax.axis_size("pos")
    mode_count = lax.axis_size("mode")
    my_mode = lax.axis_index("mode")
    share_rows = rows_tile // mode_count
    pattern = probe.shape[2]
    fr, fi = dft_tables(pattern)
    probe2 = probe[:, 0]

    before = lax.ppermute(object_field, "pos", neighbour_pairs(pos_count, 1))
    after = lax.ppermute(object_field, "pos", neighbour_pairs(pos_count, -1))
    ext_rows = 3 * rows_tile

    roff = row_offsets.astype(jnp.int32)
    coff = col_offsets.astype(jnp.int32)
    cnt = tile_counts.astype(jnp.int32)

    exits, waves, power = run_forward(before, object_field, after, probe2, fr, fi, roff, coff, cnt)
    totals = allreduce_mode(power)
    numer, illum = run_backward(
        exits, waves, totals, measured, probe2, fr, fi, roff, coff, cnt, ext_rows, width
    )

    blocks = numer.reshape(2, 3, mode_count, share_rows, width)
    blocks = jnp.sum(lax.all_to_all(blocks, "mode", 2, 2), axis=2)
    own_illum = lax.dynamic_index_in_dim(
        illum.reshape(3, mode_count, share_rows, width), my_mode, axis=1, keepdims=False
    )
    band_rows = 2 * share_rows
    to_next = jnp.concatenate([blocks[:, 2].reshape(band_rows, width), own_illum[2]], axis=0)
    to_prev = jnp.concatenate([blocks[:, 0].reshape(band_rows, width), own_illum[0]], axis=0)
    from_prev = lax.ppermute(to_next, "pos", neighbour_pairs(pos_count, 1))
    from_next = lax.ppermute(to_prev, "pos", neighbour_pairs(pos_count, -1))
    tile = (
        blocks[:, 1]
        + from_prev[:band_rows].reshape(blocks[:, 1].shape)
        + from_next[:band_rows].reshape(blocks[:, 1].shape)
    )
    illum_rows = own_illum[1] + from_prev[band_rows:] + from_next[band_rows:]

    start = my_mode * share_rows
    own_rows = lax.dynamic_slice_in_dim(object_field, start, share_rows, 1)
    return own_rows + tile / (illum_rows + 1.0)


def solution(mesh):
    in_specs = (
        P(None, "pos", None),
        P(None, "mode", None, None),
        P("pos", None, None),
        P("pos"),
        P("pos"),
        P("pos"),
    )
    out_specs = P(None, ("pos", "mode"), None)
    return jax.shard_map(local, mesh=mesh, in_specs=in_specs, out_specs=out_specs, check_vma=False)
```

```python
import math

import jax
import jax.numpy as jnp
from jax import lax
from jax.experimental import pallas as pl
from jax.experimental.pallas import tpu as pltpu
from jax.sharding import PartitionSpec as P


def dft_tables(pattern):
    counter = jnp.arange(pattern, dtype=jnp.int32)
    phases = counter[:, None] * counter[None, :] % pattern
    angles = phases.astype(jnp.float32) * (2.0 * math.pi / pattern)
    factor = 1.0 / math.sqrt(pattern)
    return (
        (jnp.cos(angles) * factor).astype(jnp.bfloat16),
        (-jnp.sin(angles) * factor).astype(jnp.bfloat16),
    )


def neighbour_pairs(size, step):
    if step > 0:
        return [(i, i + 1) for i in range(size - 1)]
    return [(i + 1, i) for i in range(size - 1)]


def mode_pairs():
    n = lax.axis_size("mode")
    chips = n // 2
    core = [(i, i ^ 1) for i in range(n)]
    near = [(i, i ^ 2) for i in range(n)]
    far = [(i, 2 * (chips - 1 - i // 2) + i % 2) for i in range(n)]
    return core, near, far


def allreduce_chips(x):
    _, near, far = mode_pairs()
    qa, qb = x[0], x[1]
    qa = qa + lax.ppermute(qa, "mode", near)
    qb = qb + lax.ppermute(qb, "mode", far)
    qa = qa + lax.ppermute(qa, "mode", far)
    qb = qb + lax.ppermute(qb, "mode", near)
    return jnp.stack([qa, qb])


def reduce_scatter_mode(x):
    core_pairs, near, far = mode_pairs()
    n = lax.axis_size("mode")
    m = lax.axis_index("mode")
    c, rows, w = x.shape
    x = x.reshape(c, 2, 2, 2, rows // n, w)
    for pairs, dim, d in ((core_pairs, 3, 1), (far, 1, 4), (near, 1, 2)):
        bit = (m // d) % 2
        keep = lax.dynamic_index_in_dim(x, bit, axis=dim, keepdims=False)
        send = lax.dynamic_index_in_dim(x, 1 - bit, axis=dim, keepdims=False)
        x = keep + lax.ppermute(send, "mode", pairs)
    return x.reshape(c, rows // n, w)


def _dot(a, b):
    return jnp.dot(a, b, preferred_element_type=jnp.float32)


def _window(ext_ref, k, r, c, pat):
    width = ext_ref.shape[2]
    base = pl.multiple_of((r // 8) * 8, 8)
    span = pat + 8
    down = (span - (r - base)) % span
    rows = pltpu.roll(ext_ref[k, pl.ds(base, span), :], down, 0)[:pat]
    return pltpu.roll(rows, (width - c) % width, 1)[:, :pat]


def _place(ref, a, r, c):
    pat = a.shape[0]
    width = ref.shape[-1]
    base = pl.multiple_of((r // 8) * 8, 8)
    span = pat + 8
    wide = pltpu.roll(jnp.concatenate([a, jnp.zeros((pat, width - pat), jnp.float32)], axis=1), c, 1)
    tall = jnp.concatenate([wide, jnp.zeros((span - pat, width), jnp.float32)], axis=0)
    ref[pl.ds(base, span), :] += pltpu.roll(tall, r - base, 0)


def forward_kernel(roff, coff, cnt, core, before_ref, own_ref, after_ref, pa_ref, pb_ref, fr_ref, fi_ref,
                   exit_ref, wave_ref, power_ref, ext_ref):
    i = pl.program_id(0)
    slots = roff.shape[0]
    pat = pa_ref.shape[1]
    band = own_ref.shape[1]
    g = core[0] + 2 * i
    gi = jnp.minimum(g, slots - 1)
    live = g < cnt[0]

    @pl.when(i == 0)
    def _():
        ext_ref[:, :band, :] = before_ref[...]
        ext_ref[:, band : 2 * band, :] = own_ref[...]
        ext_ref[:, 2 * band :, :] = after_ref[...]

    @pl.when(live)
    def _():
        r = roff[gi]
        c = coff[gi]
        obj_re = _window(ext_ref, 0, r, c, pat)
        obj_im = _window(ext_ref, 1, r, c, pat)
        fr = fr_ref[...]
        fi = fi_ref[...]
        total = None
        for k, p_ref in enumerate((pa_ref, pb_ref)):
            p_re = p_ref[0]
            p_im = p_ref[1]
            e_re = (p_re * obj_re - p_im * obj_im).astype(jnp.bfloat16)
            e_im = (p_re * obj_im + p_im * obj_re).astype(jnp.bfloat16)
            h_re = (_dot(fr, e_re) - _dot(fi, e_im)).astype(jnp.bfloat16)
            h_im = (_dot(fr, e_im) + _dot(fi, e_re)).astype(jnp.bfloat16)
            v_re = _dot(h_re, fr) - _dot(h_im, fi)
            v_im = _dot(h_re, fi) + _dot(h_im, fr)
            exit_ref[0, k, 0] = e_re
            exit_ref[0, k, 1] = e_im
            wave_ref[0, k, 0] = v_re
            wave_ref[0, k, 1] = v_im
            part = v_re * v_re + v_im * v_im
            total = part if total is None else total + part
        power_ref[i] = total

    @pl.when(g == slots)
    def _():
        total = None
        for p_ref in (pa_ref, pb_ref):
            p_re = p_ref[0]
            p_im = p_ref[1]
            part = p_re * p_re + p_im * p_im
            total = part if total is None else total + part
        power_ref[i] = total

    @pl.when(jnp.logical_and(jnp.logical_not(live), g != slots))
    def _():
        power_ref[i] = jnp.zeros((pat, pat), jnp.float32)


def backward_kernel(roff, coff, cnt, core, exit_ref, wave_ref, model_ref, meas_ref, pa_ref, pb_ref,
                    ppt_ref, fr_ref, fi_ref, numer_ref, illum_ref):
    i = pl.program_id(0)
    slots = roff.shape[0]
    g = core[0] + 2 * i
    gi = jnp.minimum(g, slots - 1)

    @pl.when(i == 0)
    def _():
        numer_ref[...] = jnp.zeros(numer_ref.shape, jnp.float32)
        illum_ref[...] = jnp.zeros(illum_ref.shape, jnp.float32)

    @pl.when(g < cnt[0])
    def _():
        r = roff[gi]
        c = coff[gi]
        scaling = jnp.sqrt(meas_ref[0]) / jnp.maximum(jnp.sqrt(model_ref[0]), 1.0)
        fr = fr_ref[...]
        fi = fi_ref[...]
        n_re = None
        n_im = None
        for k, p_ref in enumerate((pa_ref, pb_ref)):
            x_re = (scaling * wave_ref[0, k, 0]).astype(jnp.bfloat16)
            x_im = (scaling * wave_ref[0, k, 1]).astype(jnp.bfloat16)
            b_re = (_dot(fr, x_re) + _dot(fi, x_im)).astype(jnp.bfloat16)
            b_im = (_dot(fr, x_im) - _dot(fi, x_re)).astype(jnp.bfloat16)
            d_re = _dot(b_re, fr) + _dot(b_im, fi) - exit_ref[0, k, 0].astype(jnp.float32)
            d_im = _dot(b_im, fr) - _dot(b_re, fi) - exit_ref[0, k, 1].astype(jnp.float32)
            p_re = p_ref[0]
            p_im = p_ref[1]
            t_re = p_re * d_re + p_im * d_im
            t_im = p_re * d_im - p_im * d_re
            n_re = t_re if n_re is None else n_re + t_re
            n_im = t_im if n_im is None else n_im + t_im
        _place(numer_ref.at[0], n_re, r, c)
        _place(numer_ref.at[1], n_im, r, c)

    @pl.when(jnp.logical_and(core[0] == 1, i == pl.num_programs(0) - 1))
    def _():
        for slot in range(slots):
            @pl.when(slot < cnt[0])
            def _():
                _place(illum_ref, ppt_ref[0], roff[slot], coff[slot])


def run_forward(before, own, after, pa, pb, fr, fi, roff, coff, cnt, core):
    slots = roff.shape[0]
    local = (slots + 1) // 2
    pat = pa.shape[1]
    whole3 = lambda i, *_: (0, 0, 0)
    whole2 = lambda i, *_: (0, 0)
    per5 = lambda i, *_: (i, 0, 0, 0, 0)
    flops = local * 2 * 8 * 2 * pat ** 3
    ext_shape = (2, 3 * own.shape[1], own.shape[2])
    return pl.pallas_call(
        forward_kernel,
        grid_spec=pltpu.PrefetchScalarGridSpec(
            num_scalar_prefetch=4,
            grid=(local,),
            in_specs=[
                pl.BlockSpec(before.shape, whole3),
                pl.BlockSpec(own.shape, whole3),
                pl.BlockSpec(after.shape, whole3),
                pl.BlockSpec(pa.shape, whole3),
                pl.BlockSpec(pb.shape, whole3),
                pl.BlockSpec(fr.shape, whole2),
                pl.BlockSpec(fi.shape, whole2),
            ],
            out_specs=[
                pl.BlockSpec((1, 2, 2, pat, pat), per5),
                pl.BlockSpec((1, 2, 2, pat, pat), per5),
                pl.BlockSpec((local, pat, pat), whole3),
            ],
            scratch_shapes=[pltpu.VMEM(ext_shape, jnp.float32)],
        ),
        out_shape=[
            jax.ShapeDtypeStruct((local, 2, 2, pat, pat), jnp.bfloat16),
            jax.ShapeDtypeStruct((local, 2, 2, pat, pat), jnp.float32),
            jax.ShapeDtypeStruct((local, pat, pat), jnp.float32),
        ],
        compiler_params=pltpu.CompilerParams(dimension_semantics=("arbitrary",)),
        cost_estimate=pl.CostEstimate(flops=flops, transcendentals=0, bytes_accessed=10 * 1024 * 1024),
    )(roff, coff, cnt, core, before, own, after, pa, pb, fr, fi)


def run_backward(exits, waves, totals, measured, pa, pb, fr, fi, roff, coff, cnt, core, ext_rows, width):
    slots = roff.shape[0]
    local = (slots + 1) // 2
    pat = pa.shape[1]
    whole3 = lambda i, *_: (0, 0, 0)
    whole2 = lambda i, *_: (0, 0)
    per5 = lambda i, *_: (i, 0, 0, 0, 0)
    per3 = lambda i, *_: (i, 0, 0)
    slot_of = lambda i, roff, coff, cnt, core: (jnp.minimum(core[0] + 2 * i, slots - 1), 0, 0)
    flops = local * 2 * 8 * 2 * pat ** 3
    return pl.pallas_call(
        backward_kernel,
        grid_spec=pltpu.PrefetchScalarGridSpec(
            num_scalar_prefetch=4,
            grid=(local,),
            in_specs=[
                pl.BlockSpec((1, 2, 2, pat, pat), per5),
                pl.BlockSpec((1, 2, 2, pat, pat), per5),
                pl.BlockSpec((1, pat, pat), per3),
                pl.BlockSpec((1, pat, pat), slot_of),
                pl.BlockSpec(pa.shape, whole3),
                pl.BlockSpec(pb.shape, whole3),
                pl.BlockSpec((1, pat, pat), lambda i, *_: (local - 1, 0, 0)),
                pl.BlockSpec(fr.shape, whole2),
                pl.BlockSpec(fi.shape, whole2),
            ],
            out_specs=[
                pl.BlockSpec((2, ext_rows, width), whole3),
                pl.BlockSpec((ext_rows, width), whole2),
            ],
        ),
        out_shape=[
            jax.ShapeDtypeStruct((2, ext_rows, width), jnp.float32),
            jax.ShapeDtypeStruct((ext_rows, width), jnp.float32),
        ],
        compiler_params=pltpu.CompilerParams(dimension_semantics=("arbitrary",)),
        cost_estimate=pl.CostEstimate(flops=flops, transcendentals=0, bytes_accessed=14 * 1024 * 1024),
    )(roff, coff, cnt, core, exits, waves, totals, measured, pa, pb, totals, fr, fi)


def local(object_field, probe, measured, row_offsets, col_offsets, tile_counts):
    rows_tile = object_field.shape[1]
    width = object_field.shape[2]
    pos_count = lax.axis_size("pos")
    mode_count = lax.axis_size("mode")
    my_mode = lax.axis_index("mode")
    share_rows = rows_tile // mode_count
    pattern = probe.shape[2]
    fr, fi = dft_tables(pattern)
    probe2 = probe[:, 0]

    core_pairs, near, far = mode_pairs()
    core = my_mode % 2
    before = lax.ppermute(object_field, "pos", neighbour_pairs(pos_count, 1))
    after = lax.ppermute(object_field, "pos", neighbour_pairs(pos_count, -1))
    partner_probe = lax.ppermute(probe2, "mode", core_pairs)
    ext_rows = 3 * rows_tile

    roff = row_offsets.astype(jnp.int32)
    coff = col_offsets.astype(jnp.int32)
    cnt = tile_counts.astype(jnp.int32)
    core_arr = jnp.reshape(core, (1,)).astype(jnp.int32)

    exits, waves, power = run_forward(
        before, object_field, after, probe2, partner_probe, fr, fi, roff, coff, cnt, core_arr
    )
    totals = allreduce_chips(power)
    numer, illum = run_backward(
        exits, waves, totals, measured, probe2, partner_probe, fr, fi, roff, coff, cnt, core_arr,
        ext_rows, width
    )

    blocks = numer.reshape(2, 3, 2, 2, 2, share_rows, width)
    keep = lax.dynamic_index_in_dim(blocks, core, axis=4, keepdims=False)
    send = lax.dynamic_index_in_dim(blocks, 1 - core, axis=4, keepdims=False)
    illum_blocks = illum.reshape(3, mode_count, share_rows, width)
    partner = my_mode + 1 - 2 * core
    illum_partner = lax.dynamic_index_in_dim(illum_blocks, partner, axis=1, keepdims=False)
    numer_rows = send.size // width
    message = jnp.concatenate(
        [send.reshape(numer_rows, width), illum_partner.reshape(-1, width)], axis=0
    )
    got = lax.ppermute(message, "mode", core_pairs)
    blocks = keep + got[:numer_rows].reshape(keep.shape)
    own_illum = lax.dynamic_index_in_dim(illum_blocks, my_mode, axis=1, keepdims=False)
    own_illum = own_illum + got[numer_rows:].reshape(own_illum.shape)
    band_rows = 2 * 4 * share_rows
    to_next = jnp.concatenate([blocks[:, 2].reshape(band_rows, width), own_illum[2]], axis=0)
    to_prev = jnp.concatenate([blocks[:, 0].reshape(band_rows, width), own_illum[0]], axis=0)
    from_prev = lax.ppermute(to_next, "pos", neighbour_pairs(pos_count, 1))
    from_next = lax.ppermute(to_prev, "pos", neighbour_pairs(pos_count, -1))
    tile = (
        blocks[:, 1]
        + from_prev[:band_rows].reshape(blocks[:, 1].shape)
        + from_next[:band_rows].reshape(blocks[:, 1].shape)
    )
    illum_rows = own_illum[1] + from_prev[band_rows:] + from_next[band_rows:]
    for pairs, d in ((far, 4), (near, 2)):
        bit = (my_mode // d) % 2
        keep = lax.dynamic_index_in_dim(tile, bit, axis=1, keepdims=False)
        send = lax.dynamic_index_in_dim(tile, 1 - bit, axis=1, keepdims=False)
        tile = keep + lax.ppermute(send, "mode", pairs)

    start = my_mode * share_rows
    own_rows = lax.dynamic_slice_in_dim(object_field, start, share_rows, 1)
    return own_rows + tile / (illum_rows + 1.0)


def solution(mesh):
    in_specs = (
        P(None, "pos", None),
        P(None, "mode", None, None),
        P("pos", None, None),
        P("pos"),
        P("pos"),
        P("pos"),
    )
    out_specs = P(None, ("pos", "mode"), None)
    return jax.shard_map(local, mesh=mesh, in_specs=in_specs, out_specs=out_specs, check_vma=False)
```

```python
import math

import jax
import jax.numpy as jnp
from jax import lax
from jax.experimental import pallas as pl
from jax.experimental.pallas import tpu as pltpu
from jax.sharding import PartitionSpec as P


def dft_tables(pattern):
    counter = jnp.arange(pattern, dtype=jnp.int32)
    phases = counter[:, None] * counter[None, :] % pattern
    angles = phases.astype(jnp.float32) * (2.0 * math.pi / pattern)
    factor = 1.0 / math.sqrt(pattern)
    return (
        (jnp.cos(angles) * factor).astype(jnp.bfloat16),
        (-jnp.sin(angles) * factor).astype(jnp.bfloat16),
    )


def neighbour_pairs(size, step):
    if step > 0:
        return [(i, i + 1) for i in range(size - 1)]
    return [(i + 1, i) for i in range(size - 1)]


def mode_pairs():
    n = lax.axis_size("mode")
    chips = n // 2
    core = [(i, i ^ 1) for i in range(n)]
    near = [(i, i ^ 2) for i in range(n)]
    far = [(i, 2 * (chips - 1 - i // 2) + i % 2) for i in range(n)]
    return core, near, far


def allreduce_chips(qa, qb):
    _, near, far = mode_pairs()
    qa = qa + lax.ppermute(qa, "mode", near)
    qb = qb + lax.ppermute(qb, "mode", far)
    qa = qa + lax.ppermute(qa, "mode", far)
    qb = qb + lax.ppermute(qb, "mode", near)
    return qa, qb


def reduce_scatter_mode(x):
    core_pairs, near, far = mode_pairs()
    n = lax.axis_size("mode")
    m = lax.axis_index("mode")
    c, rows, w = x.shape
    x = x.reshape(c, 2, 2, 2, rows // n, w)
    for pairs, dim, d in ((core_pairs, 3, 1), (far, 1, 4), (near, 1, 2)):
        bit = (m // d) % 2
        keep = lax.dynamic_index_in_dim(x, bit, axis=dim, keepdims=False)
        send = lax.dynamic_index_in_dim(x, 1 - bit, axis=dim, keepdims=False)
        x = keep + lax.ppermute(send, "mode", pairs)
    return x.reshape(c, rows // n, w)


def _dot(a, b):
    return jnp.dot(a, b, preferred_element_type=jnp.float32)


def _window(ext_ref, k, r, c, pat):
    width = ext_ref.shape[2]
    base = pl.multiple_of((r // 8) * 8, 8)
    span = pat + 8
    down = (span - (r - base)) % span
    rows = pltpu.roll(ext_ref[k, pl.ds(base, span), :], down, 0)[:pat]
    return pltpu.roll(rows, (width - c) % width, 1)[:, :pat]


def _place(ref, a, r, c):
    pat = a.shape[0]
    width = ref.shape[-1]
    base = pl.multiple_of((r // 8) * 8, 8)
    span = pat + 8
    wide = pltpu.roll(jnp.concatenate([a, jnp.zeros((pat, width - pat), jnp.float32)], axis=1), c, 1)
    tall = jnp.concatenate([wide, jnp.zeros((span - pat, width), jnp.float32)], axis=0)
    ref[pl.ds(base, span), :] += pltpu.roll(tall, r - base, 0)


def forward_kernel(roff, coff, cnt, core, before_ref, own_ref, after_ref, pa_ref, pb_ref, fr_ref, fi_ref,
                   exit_ref, wave_ref, power_a_ref, power_b_ref, ext_ref):
    i = pl.program_id(0)
    slots = roff.shape[0]
    pat = pa_ref.shape[1]
    band = own_ref.shape[1]
    g = core[0] + 2 * i
    gi = jnp.minimum(g, slots - 1)
    live = g < cnt[0]

    def store_power(value):
        @pl.when(i == 0)
        def _():
            power_a_ref[...] = value

        @pl.when(i == 1)
        def _():
            power_b_ref[...] = value

    @pl.when(i == 0)
    def _():
        ext_ref[:, :band, :] = before_ref[...]
        ext_ref[:, band : 2 * band, :] = own_ref[...]
        ext_ref[:, 2 * band :, :] = after_ref[...]

    @pl.when(live)
    def _():
        r = roff[gi]
        c = coff[gi]
        obj_re = _window(ext_ref, 0, r, c, pat)
        obj_im = _window(ext_ref, 1, r, c, pat)
        fr = fr_ref[...]
        fi = fi_ref[...]
        total = None
        for k, p_ref in enumerate((pa_ref, pb_ref)):
            p_re = p_ref[0]
            p_im = p_ref[1]
            e_re = (p_re * obj_re - p_im * obj_im).astype(jnp.bfloat16)
            e_im = (p_re * obj_im + p_im * obj_re).astype(jnp.bfloat16)
            h_re = (_dot(fr, e_re) - _dot(fi, e_im)).astype(jnp.bfloat16)
            h_im = (_dot(fr, e_im) + _dot(fi, e_re)).astype(jnp.bfloat16)
            v_re = _dot(h_re, fr) - _dot(h_im, fi)
            v_im = _dot(h_re, fi) + _dot(h_im, fr)
            exit_ref[0, k, 0] = e_re
            exit_ref[0, k, 1] = e_im
            wave_ref[0, k, 0] = v_re
            wave_ref[0, k, 1] = v_im
            part = v_re * v_re + v_im * v_im
            total = part if total is None else total + part
        store_power(total)

    @pl.when(g == slots)
    def _():
        total = None
        for p_ref in (pa_ref, pb_ref):
            p_re = p_ref[0]
            p_im = p_ref[1]
            part = p_re * p_re + p_im * p_im
            total = part if total is None else total + part
        store_power(total)

    @pl.when(jnp.logical_and(jnp.logical_not(live), g != slots))
    def _():
        store_power(jnp.zeros((pat, pat), jnp.float32))


def backward_kernel(roff, coff, cnt, core, exit_ref, wave_ref, ma_ref, mb_ref, meas_ref, pa_ref, pb_ref,
                    fr_ref, fi_ref, keep_ref, message_ref, own_illum_ref, numer_ref, illum_ref):
    i = pl.program_id(0)
    last = pl.num_programs(0) - 1
    slots = roff.shape[0]
    g = core[0] + 2 * i
    gi = jnp.minimum(g, slots - 1)

    @pl.when(i == 0)
    def _():
        numer_ref[...] = jnp.zeros(numer_ref.shape, jnp.float32)
        illum_ref[...] = jnp.zeros(illum_ref.shape, jnp.float32)

    @pl.when(g < cnt[0])
    def _():
        r = roff[gi]
        c = coff[gi]
        model = jnp.where(i == 0, ma_ref[...], mb_ref[...])
        scaling = jnp.sqrt(meas_ref[0]) / jnp.maximum(jnp.sqrt(model), 1.0)
        fr = fr_ref[...]
        fi = fi_ref[...]
        n_re = None
        n_im = None
        for k, p_ref in enumerate((pa_ref, pb_ref)):
            x_re = (scaling * wave_ref[0, k, 0]).astype(jnp.bfloat16)
            x_im = (scaling * wave_ref[0, k, 1]).astype(jnp.bfloat16)
            b_re = (_dot(fr, x_re) + _dot(fi, x_im)).astype(jnp.bfloat16)
            b_im = (_dot(fr, x_im) - _dot(fi, x_re)).astype(jnp.bfloat16)
            d_re = _dot(b_re, fr) + _dot(b_im, fi) - exit_ref[0, k, 0].astype(jnp.float32)
            d_im = _dot(b_im, fr) - _dot(b_re, fi) - exit_ref[0, k, 1].astype(jnp.float32)
            p_re = p_ref[0]
            p_im = p_ref[1]
            t_re = p_re * d_re + p_im * d_im
            t_im = p_re * d_im - p_im * d_re
            n_re = t_re if n_re is None else n_re + t_re
            n_im = t_im if n_im is None else n_im + t_im
        _place(numer_ref.at[0], n_re, r, c)
        _place(numer_ref.at[1], n_im, r, c)

    @pl.when(jnp.logical_and(core[0] == 1, i == last))
    def _():
        for slot in range(slots):
            @pl.when(slot < cnt[0])
            def _():
                _place(illum_ref, mb_ref[...], roff[slot], coff[slot])

    @pl.when(i == last)
    def _():
        side = core[0]
        mode = core[1]
        partner = mode + 1 - 2 * side
        band = numer_ref.shape[1] // 3
        share = band // 8
        quads = 4
        for ch in range(2):
            for b in range(3):
                for q in range(quads):
                    dst = ((ch * 3 + b) * quads + q) * share
                    kept = pl.multiple_of(b * band + (2 * q + side) * share, 8)
                    sent = pl.multiple_of(b * band + (2 * q + 1 - side) * share, 8)
                    keep_ref[dst : dst + share, :] = numer_ref[ch, pl.ds(kept, share), :]
                    message_ref[dst : dst + share, :] = numer_ref[ch, pl.ds(sent, share), :]
        top = 2 * 3 * quads * share
        for b in range(3):
            theirs = pl.multiple_of(b * band + partner * share, 8)
            mine = pl.multiple_of(b * band + mode * share, 8)
            message_ref[top + b * share : top + (b + 1) * share, :] = illum_ref[pl.ds(theirs, share), :]
            own_illum_ref[b * share : (b + 1) * share, :] = illum_ref[pl.ds(mine, share), :]


def run_forward(before, own, after, pa, pb, fr, fi, roff, coff, cnt, core):
    slots = roff.shape[0]
    local = (slots + 1) // 2
    pat = pa.shape[1]
    whole3 = lambda i, *_: (0, 0, 0)
    whole2 = lambda i, *_: (0, 0)
    per5 = lambda i, *_: (i, 0, 0, 0, 0)
    flops = local * 2 * 8 * 2 * pat ** 3
    ext_shape = (2, 3 * own.shape[1], own.shape[2])
    return pl.pallas_call(
        forward_kernel,
        grid_spec=pltpu.PrefetchScalarGridSpec(
            num_scalar_prefetch=4,
            grid=(local,),
            in_specs=[
                pl.BlockSpec(before.shape, whole3),
                pl.BlockSpec(own.shape, whole3),
                pl.BlockSpec(after.shape, whole3),
                pl.BlockSpec(pa.shape, whole3),
                pl.BlockSpec(pb.shape, whole3),
                pl.BlockSpec(fr.shape, whole2),
                pl.BlockSpec(fi.shape, whole2),
            ],
            out_specs=[
                pl.BlockSpec((1, 2, 2, pat, pat), per5),
                pl.BlockSpec((1, 2, 2, pat, pat), per5),
                pl.BlockSpec((pat, pat), whole2),
                pl.BlockSpec((pat, pat), whole2),
            ],
            scratch_shapes=[pltpu.VMEM(ext_shape, jnp.float32)],
        ),
        out_shape=[
            jax.ShapeDtypeStruct((local, 2, 2, pat, pat), jnp.bfloat16),
            jax.ShapeDtypeStruct((local, 2, 2, pat, pat), jnp.float32),
            jax.ShapeDtypeStruct((pat, pat), jnp.float32),
            jax.ShapeDtypeStruct((pat, pat), jnp.float32),
        ],
        compiler_params=pltpu.CompilerParams(dimension_semantics=("arbitrary",)),
        cost_estimate=pl.CostEstimate(flops=flops, transcendentals=0, bytes_accessed=10 * 1024 * 1024),
    )(roff, coff, cnt, core, before, own, after, pa, pb, fr, fi)


def run_backward(exits, waves, model_a, model_b, measured, pa, pb, fr, fi, roff, coff, cnt, ids,
                 ext_rows, width):
    slots = roff.shape[0]
    local = (slots + 1) // 2
    pat = pa.shape[1]
    share = ext_rows // 3 // 8
    kept_rows = 2 * ext_rows // 2
    whole3 = lambda i, *_: (0, 0, 0)
    whole2 = lambda i, *_: (0, 0)
    per5 = lambda i, *_: (i, 0, 0, 0, 0)
    slot_of = lambda i, roff, coff, cnt, core: (jnp.minimum(core[0] + 2 * i, slots - 1), 0, 0)
    flops = local * 2 * 8 * 2 * pat ** 3
    return pl.pallas_call(
        backward_kernel,
        grid_spec=pltpu.PrefetchScalarGridSpec(
            num_scalar_prefetch=4,
            grid=(local,),
            in_specs=[
                pl.BlockSpec((1, 2, 2, pat, pat), per5),
                pl.BlockSpec((1, 2, 2, pat, pat), per5),
                pl.BlockSpec((pat, pat), whole2),
                pl.BlockSpec((pat, pat), whole2),
                pl.BlockSpec((1, pat, pat), slot_of),
                pl.BlockSpec(pa.shape, whole3),
                pl.BlockSpec(pb.shape, whole3),
                pl.BlockSpec(fr.shape, whole2),
                pl.BlockSpec(fi.shape, whole2),
            ],
            out_specs=[
                pl.BlockSpec((kept_rows, width), whole2),
                pl.BlockSpec((kept_rows + 3 * share, width), whole2),
                pl.BlockSpec((3 * share, width), whole2),
            ],
            scratch_shapes=[
                pltpu.VMEM((2, ext_rows, width), jnp.float32),
                pltpu.VMEM((ext_rows, width), jnp.float32),
            ],
        ),
        out_shape=[
            jax.ShapeDtypeStruct((kept_rows, width), jnp.float32),
            jax.ShapeDtypeStruct((kept_rows + 3 * share, width), jnp.float32),
            jax.ShapeDtypeStruct((3 * share, width), jnp.float32),
        ],
        compiler_params=pltpu.CompilerParams(dimension_semantics=("arbitrary",)),
        cost_estimate=pl.CostEstimate(flops=flops, transcendentals=0, bytes_accessed=12 * 1024 * 1024),
    )(roff, coff, cnt, ids, exits, waves, model_a, model_b, measured, pa, pb, fr, fi)


def local(object_field, probe, measured, row_offsets, col_offsets, tile_counts):
    rows_tile = object_field.shape[1]
    width = object_field.shape[2]
    pos_count = lax.axis_size("pos")
    mode_count = lax.axis_size("mode")
    my_mode = lax.axis_index("mode")
    share_rows = rows_tile // mode_count
    pattern = probe.shape[2]
    fr, fi = dft_tables(pattern)
    probe2 = probe[:, 0]

    core_pairs, near, far = mode_pairs()
    core = my_mode % 2
    before = lax.ppermute(object_field, "pos", neighbour_pairs(pos_count, 1))
    after = lax.ppermute(object_field, "pos", neighbour_pairs(pos_count, -1))
    partner_probe = lax.ppermute(probe2, "mode", core_pairs)
    ext_rows = 3 * rows_tile

    roff = row_offsets.astype(jnp.int32)
    coff = col_offsets.astype(jnp.int32)
    cnt = tile_counts.astype(jnp.int32)
    ids = jnp.stack([core, my_mode]).astype(jnp.int32)

    exits, waves, power_a, power_b = run_forward(
        before, object_field, after, probe2, partner_probe, fr, fi, roff, coff, cnt, ids
    )
    model_a, model_b = allreduce_chips(power_a, power_b)
    kept, message, own_illum = run_backward(
        exits, waves, model_a, model_b, measured, probe2, partner_probe, fr, fi, roff, coff, cnt, ids,
        ext_rows, width
    )

    got = lax.ppermute(message, "mode", core_pairs)
    numer_rows = kept.shape[0]
    block_shape = (2, 3, 2, 2, share_rows, width)
    blocks = kept.reshape(block_shape) + got[:numer_rows].reshape(block_shape)
    own_illum = own_illum.reshape(3, share_rows, width) + got[numer_rows:].reshape(3, share_rows, width)
    band_rows = 2 * 4 * share_rows
    to_next = jnp.concatenate([blocks[:, 2].reshape(band_rows, width), own_illum[2]], axis=0)
    to_prev = jnp.concatenate([blocks[:, 0].reshape(band_rows, width), own_illum[0]], axis=0)
    from_prev = lax.ppermute(to_next, "pos", neighbour_pairs(pos_count, 1))
    from_next = lax.ppermute(to_prev, "pos", neighbour_pairs(pos_count, -1))
    tile = (
        blocks[:, 1]
        + from_prev[:band_rows].reshape(blocks[:, 1].shape)
        + from_next[:band_rows].reshape(blocks[:, 1].shape)
    )
    illum_rows = own_illum[1] + from_prev[band_rows:] + from_next[band_rows:]
    for pairs, d in ((far, 4), (near, 2)):
        bit = (my_mode // d) % 2
        keep = lax.dynamic_index_in_dim(tile, bit, axis=1, keepdims=False)
        send = lax.dynamic_index_in_dim(tile, 1 - bit, axis=1, keepdims=False)
        tile = keep + lax.ppermute(send, "mode", pairs)

    start = my_mode * share_rows
    own_rows = lax.dynamic_slice_in_dim(object_field, start, share_rows, 1)
    return own_rows + tile / (illum_rows + 1.0)


def solution(mesh):
    in_specs = (
        P(None, "pos", None),
        P(None, "mode", None, None),
        P("pos", None, None),
        P("pos"),
        P("pos"),
        P("pos"),
    )
    out_specs = P(None, ("pos", "mode"), None)
    return jax.shard_map(local, mesh=mesh, in_specs=in_specs, out_specs=out_specs, check_vma=False)
```

```python
import math

import jax
import jax.numpy as jnp
from jax import lax
from jax.experimental import pallas as pl
from jax.experimental.pallas import tpu as pltpu
from jax.sharding import PartitionSpec as P


def dft_tables(pattern):
    counter = jnp.arange(pattern, dtype=jnp.int32)
    phases = counter[:, None] * counter[None, :] % pattern
    angles = phases.astype(jnp.float32) * (2.0 * math.pi / pattern)
    factor = 1.0 / math.sqrt(pattern)
    return (
        (jnp.cos(angles) * factor).astype(jnp.bfloat16),
        (-jnp.sin(angles) * factor).astype(jnp.bfloat16),
    )


def neighbour_pairs(size, step):
    if step > 0:
        return [(i, i + 1) for i in range(size - 1)]
    return [(i + 1, i) for i in range(size - 1)]


def mode_pairs():
    n = lax.axis_size("mode")
    chips = n // 2
    core = [(i, i ^ 1) for i in range(n)]
    near = [(i, i ^ 2) for i in range(n)]
    far = [(i, 2 * (chips - 1 - i // 2) + i % 2) for i in range(n)]
    return core, near, far


def allreduce_chips(qa, qb):
    _, near, far = mode_pairs()
    qa = qa + lax.ppermute(qa, "mode", near)
    qb = qb + lax.ppermute(qb, "mode", far)
    qa = qa + lax.ppermute(qa, "mode", far)
    qb = qb + lax.ppermute(qb, "mode", near)
    return qa, qb


def reduce_scatter_mode(x):
    core_pairs, near, far = mode_pairs()
    n = lax.axis_size("mode")
    m = lax.axis_index("mode")
    c, rows, w = x.shape
    x = x.reshape(c, 2, 2, 2, rows // n, w)
    for pairs, dim, d in ((core_pairs, 3, 1), (far, 1, 4), (near, 1, 2)):
        bit = (m // d) % 2
        keep = lax.dynamic_index_in_dim(x, bit, axis=dim, keepdims=False)
        send = lax.dynamic_index_in_dim(x, 1 - bit, axis=dim, keepdims=False)
        x = keep + lax.ppermute(send, "mode", pairs)
    return x.reshape(c, rows // n, w)


def _dot(a, b):
    return jnp.dot(a, b, preferred_element_type=jnp.float32)


def _window(ext_ref, k, r, c, pat):
    width = ext_ref.shape[2]
    base = pl.multiple_of((r // 8) * 8, 8)
    span = pat + 8
    down = (span - (r - base)) % span
    rows = pltpu.roll(ext_ref[k, pl.ds(base, span), :], down, 0)[:pat]
    return pltpu.roll(rows, (width - c) % width, 1)[:, :pat]


def _place(ref, a, r, c):
    pat = a.shape[0]
    width = ref.shape[-1]
    base = pl.multiple_of((r // 8) * 8, 8)
    span = pat + 8
    wide = pltpu.roll(jnp.concatenate([a, jnp.zeros((pat, width - pat), jnp.float32)], axis=1), c, 1)
    tall = jnp.concatenate([wide, jnp.zeros((span - pat, width), jnp.float32)], axis=0)
    ref[pl.ds(base, span), :] += pltpu.roll(tall, r - base, 0)


def forward_kernel(roff, coff, cnt, core, before_ref, own_ref, after_ref, pa_ref, pb_ref, fr_ref, fi_ref,
                   exit_ref, wave_ref, power_a_ref, power_b_ref, ext_ref):
    i = pl.program_id(0)
    slots = roff.shape[0]
    pat = pa_ref.shape[1]
    band = own_ref.shape[1]
    g = core[0] + 2 * i
    gi = jnp.minimum(g, slots - 1)
    live = g < cnt[0]

    def store_power(value):
        @pl.when(i == 0)
        def _():
            power_a_ref[...] = value

        @pl.when(i == 1)
        def _():
            power_b_ref[...] = value

    @pl.when(i == 0)
    def _():
        ext_ref[:, :band, :] = before_ref[...]
        ext_ref[:, band : 2 * band, :] = own_ref[...]
        ext_ref[:, 2 * band :, :] = after_ref[...]

    @pl.when(live)
    def _():
        r = roff[gi]
        c = coff[gi]
        obj_re = _window(ext_ref, 0, r, c, pat)
        obj_im = _window(ext_ref, 1, r, c, pat)
        fr = fr_ref[...]
        fi = fi_ref[...]
        total = None
        for k, p_ref in enumerate((pa_ref, pb_ref)):
            p_re = p_ref[0]
            p_im = p_ref[1]
            e_re = (p_re * obj_re - p_im * obj_im).astype(jnp.bfloat16)
            e_im = (p_re * obj_im + p_im * obj_re).astype(jnp.bfloat16)
            h_re = (_dot(fr, e_re) - _dot(fi, e_im)).astype(jnp.bfloat16)
            h_im = (_dot(fr, e_im) + _dot(fi, e_re)).astype(jnp.bfloat16)
            v_re = _dot(h_re, fr) - _dot(h_im, fi)
            v_im = _dot(h_re, fi) + _dot(h_im, fr)
            exit_ref[0, k, 0] = e_re
            exit_ref[0, k, 1] = e_im
            wave_ref[0, k, 0] = v_re
            wave_ref[0, k, 1] = v_im
            part = v_re * v_re + v_im * v_im
            total = part if total is None else total + part
        store_power(total)

    @pl.when(g == slots)
    def _():
        total = None
        for p_ref in (pa_ref, pb_ref):
            p_re = p_ref[0]
            p_im = p_ref[1]
            part = p_re * p_re + p_im * p_im
            total = part if total is None else total + part
        store_power(total)

    @pl.when(jnp.logical_and(jnp.logical_not(live), g != slots))
    def _():
        store_power(jnp.zeros((pat, pat), jnp.float32))


def backward_kernel(roff, coff, cnt, core, exit_ref, wave_ref, ma_ref, mb_ref, meas_ref, pa_ref, pb_ref,
                    fr_ref, fi_ref, keep_ref, message_ref, own_illum_ref, numer_ref, illum_ref):
    i = pl.program_id(0)
    last = pl.num_programs(0) - 1
    slots = roff.shape[0]
    g = core[0] + 2 * i
    gi = jnp.minimum(g, slots - 1)

    @pl.when(i == 0)
    def _():
        numer_ref[...] = jnp.zeros(numer_ref.shape, jnp.float32)
        illum_ref[...] = jnp.zeros(illum_ref.shape, jnp.float32)

    @pl.when(g < cnt[0])
    def _():
        r = roff[gi]
        c = coff[gi]
        model = jnp.where(i == 0, ma_ref[...], mb_ref[...])
        scaling = jnp.sqrt(meas_ref[0]) / jnp.maximum(jnp.sqrt(model), 1.0)
        fr = fr_ref[...]
        fi = fi_ref[...]
        n_re = None
        n_im = None
        for k, p_ref in enumerate((pa_ref, pb_ref)):
            x_re = (scaling * wave_ref[0, k, 0]).astype(jnp.bfloat16)
            x_im = (scaling * wave_ref[0, k, 1]).astype(jnp.bfloat16)
            b_re = (_dot(fr, x_re) + _dot(fi, x_im)).astype(jnp.bfloat16)
            b_im = (_dot(fr, x_im) - _dot(fi, x_re)).astype(jnp.bfloat16)
            d_re = _dot(b_re, fr) + _dot(b_im, fi) - exit_ref[0, k, 0].astype(jnp.float32)
            d_im = _dot(b_im, fr) - _dot(b_re, fi) - exit_ref[0, k, 1].astype(jnp.float32)
            p_re = p_ref[0]
            p_im = p_ref[1]
            t_re = p_re * d_re + p_im * d_im
            t_im = p_re * d_im - p_im * d_re
            n_re = t_re if n_re is None else n_re + t_re
            n_im = t_im if n_im is None else n_im + t_im
        _place(numer_ref.at[0], n_re, r, c)
        _place(numer_ref.at[1], n_im, r, c)

    @pl.when(jnp.logical_and(core[0] == 1, i == last))
    def _():
        for slot in range(slots):
            @pl.when(slot < cnt[0])
            def _():
                _place(illum_ref, mb_ref[...], roff[slot], coff[slot])

    @pl.when(i == last)
    def _():
        side = core[0]
        mode = core[1]
        partner = mode + 1 - 2 * side
        band = numer_ref.shape[1] // 3
        share = band // 8
        quads = 4
        for ch in range(2):
            for b in range(3):
                for q in range(quads):
                    dst = ((ch * 3 + b) * quads + q) * share
                    kept = pl.multiple_of(b * band + (2 * q + side) * share, 8)
                    sent = pl.multiple_of(b * band + (2 * q + 1 - side) * share, 8)
                    keep_ref[dst : dst + share, :] = numer_ref[ch, pl.ds(kept, share), :]
                    message_ref[dst : dst + share, :] = numer_ref[ch, pl.ds(sent, share), :]
        top = 2 * 3 * quads * share
        for b in range(3):
            theirs = pl.multiple_of(b * band + partner * share, 8)
            mine = pl.multiple_of(b * band + mode * share, 8)
            message_ref[top + b * share : top + (b + 1) * share, :] = illum_ref[pl.ds(theirs, share), :]
            own_illum_ref[b * share : (b + 1) * share, :] = illum_ref[pl.ds(mine, share), :]


def run_forward(before, own, after, pa, pb, fr, fi, roff, coff, cnt, core):
    slots = roff.shape[0]
    local = (slots + 1) // 2
    pat = pa.shape[1]
    whole3 = lambda i, *_: (0, 0, 0)
    whole2 = lambda i, *_: (0, 0)
    per5 = lambda i, *_: (i, 0, 0, 0, 0)
    flops = local * 2 * 8 * 2 * pat ** 3
    ext_shape = (2, 3 * own.shape[1], own.shape[2])
    return pl.pallas_call(
        forward_kernel,
        grid_spec=pltpu.PrefetchScalarGridSpec(
            num_scalar_prefetch=4,
            grid=(local,),
            in_specs=[
                pl.BlockSpec(before.shape, whole3),
                pl.BlockSpec(own.shape, whole3),
                pl.BlockSpec(after.shape, whole3),
                pl.BlockSpec(pa.shape, whole3),
                pl.BlockSpec(pb.shape, whole3),
                pl.BlockSpec(fr.shape, whole2),
                pl.BlockSpec(fi.shape, whole2),
            ],
            out_specs=[
                pl.BlockSpec((1, 2, 2, pat, pat), per5),
                pl.BlockSpec((1, 2, 2, pat, pat), per5),
                pl.BlockSpec((pat, pat), whole2),
                pl.BlockSpec((pat, pat), whole2),
            ],
            scratch_shapes=[pltpu.VMEM(ext_shape, jnp.float32)],
        ),
        out_shape=[
            jax.ShapeDtypeStruct((local, 2, 2, pat, pat), jnp.bfloat16),
            jax.ShapeDtypeStruct((local, 2, 2, pat, pat), jnp.float32),
            jax.ShapeDtypeStruct((pat, pat), jnp.float32),
            jax.ShapeDtypeStruct((pat, pat), jnp.float32),
        ],
        compiler_params=pltpu.CompilerParams(dimension_semantics=("arbitrary",)),
        cost_estimate=pl.CostEstimate(flops=flops, transcendentals=0, bytes_accessed=10 * 1024 * 1024),
    )(roff, coff, cnt, core, before, own, after, pa, pb, fr, fi)


def run_backward(exits, waves, model_a, model_b, measured, pa, pb, fr, fi, roff, coff, cnt, ids,
                 ext_rows, width):
    slots = roff.shape[0]
    local = (slots + 1) // 2
    pat = pa.shape[1]
    share = ext_rows // 3 // 8
    kept_rows = 2 * ext_rows // 2
    whole3 = lambda i, *_: (0, 0, 0)
    whole2 = lambda i, *_: (0, 0)
    per5 = lambda i, *_: (i, 0, 0, 0, 0)
    slot_of = lambda i, roff, coff, cnt, core: (jnp.minimum(core[0] + 2 * i, slots - 1), 0, 0)
    flops = local * 2 * 8 * 2 * pat ** 3
    return pl.pallas_call(
        backward_kernel,
        grid_spec=pltpu.PrefetchScalarGridSpec(
            num_scalar_prefetch=4,
            grid=(local,),
            in_specs=[
                pl.BlockSpec((1, 2, 2, pat, pat), per5),
                pl.BlockSpec((1, 2, 2, pat, pat), per5),
                pl.BlockSpec((pat, pat), whole2),
                pl.BlockSpec((pat, pat), whole2),
                pl.BlockSpec((1, pat, pat), slot_of),
                pl.BlockSpec(pa.shape, whole3),
                pl.BlockSpec(pb.shape, whole3),
                pl.BlockSpec(fr.shape, whole2),
                pl.BlockSpec(fi.shape, whole2),
            ],
            out_specs=[
                pl.BlockSpec((kept_rows, width), whole2),
                pl.BlockSpec((kept_rows + 3 * share, width), whole2),
                pl.BlockSpec((3 * share, width), whole2),
            ],
            scratch_shapes=[
                pltpu.VMEM((2, ext_rows, width), jnp.float32),
                pltpu.VMEM((ext_rows, width), jnp.float32),
            ],
        ),
        out_shape=[
            jax.ShapeDtypeStruct((kept_rows, width), jnp.float32),
            jax.ShapeDtypeStruct((kept_rows + 3 * share, width), jnp.float32),
            jax.ShapeDtypeStruct((3 * share, width), jnp.float32),
        ],
        compiler_params=pltpu.CompilerParams(dimension_semantics=("arbitrary",)),
        cost_estimate=pl.CostEstimate(flops=flops, transcendentals=0, bytes_accessed=12 * 1024 * 1024),
    )(roff, coff, cnt, ids, exits, waves, model_a, model_b, measured, pa, pb, fr, fi)


def local(object_field, probe, measured, row_offsets, col_offsets, tile_counts):
    rows_tile = object_field.shape[1]
    width = object_field.shape[2]
    pos_count = lax.axis_size("pos")
    mode_count = lax.axis_size("mode")
    my_mode = lax.axis_index("mode")
    share_rows = rows_tile // mode_count
    pattern = probe.shape[2]
    fr, fi = dft_tables(pattern)
    probe2 = probe[:, 0]

    core_pairs, near, far = mode_pairs()
    core = my_mode % 2
    before = lax.ppermute(object_field, "pos", neighbour_pairs(pos_count, 1))
    after = lax.ppermute(object_field, "pos", neighbour_pairs(pos_count, -1))
    probe_late, before = lax.optimization_barrier((probe2, before))
    partner_probe = lax.ppermute(probe_late, "mode", core_pairs)
    ext_rows = 3 * rows_tile

    roff = row_offsets.astype(jnp.int32)
    coff = col_offsets.astype(jnp.int32)
    cnt = tile_counts.astype(jnp.int32)
    ids = jnp.stack([core, my_mode]).astype(jnp.int32)

    exits, waves, power_a, power_b = run_forward(
        before, object_field, after, probe2, partner_probe, fr, fi, roff, coff, cnt, ids
    )
    model_a, model_b = allreduce_chips(power_a, power_b)
    kept, message, own_illum = run_backward(
        exits, waves, model_a, model_b, measured, probe2, partner_probe, fr, fi, roff, coff, cnt, ids,
        ext_rows, width
    )

    got = lax.ppermute(message, "mode", core_pairs)
    numer_rows = kept.shape[0]
    block_shape = (2, 3, 2, 2, share_rows, width)
    blocks = kept.reshape(block_shape) + got[:numer_rows].reshape(block_shape)
    own_illum = own_illum.reshape(3, share_rows, width) + got[numer_rows:].reshape(3, share_rows, width)
    band_rows = 2 * 4 * share_rows
    to_next = jnp.concatenate([blocks[:, 2].reshape(band_rows, width), own_illum[2]], axis=0)
    to_prev = jnp.concatenate([blocks[:, 0].reshape(band_rows, width), own_illum[0]], axis=0)
    from_prev = lax.ppermute(to_next, "pos", neighbour_pairs(pos_count, 1))
    from_next = lax.ppermute(to_prev, "pos", neighbour_pairs(pos_count, -1))
    tile = (
        blocks[:, 1]
        + from_prev[:band_rows].reshape(blocks[:, 1].shape)
        + from_next[:band_rows].reshape(blocks[:, 1].shape)
    )
    illum_rows = own_illum[1] + from_prev[band_rows:] + from_next[band_rows:]
    for pairs, d in ((far, 4), (near, 2)):
        bit = (my_mode // d) % 2
        keep = lax.dynamic_index_in_dim(tile, bit, axis=1, keepdims=False)
        send = lax.dynamic_index_in_dim(tile, 1 - bit, axis=1, keepdims=False)
        tile = keep + lax.ppermute(send, "mode", pairs)

    start = my_mode * share_rows
    own_rows = lax.dynamic_slice_in_dim(object_field, start, share_rows, 1)
    return own_rows + tile / (illum_rows + 1.0)


def solution(mesh):
    in_specs = (
        P(None, "pos", None),
        P(None, "mode", None, None),
        P("pos", None, None),
        P("pos"),
        P("pos"),
        P("pos"),
    )
    out_specs = P(None, ("pos", "mode"), None)
    return jax.shard_map(local, mesh=mesh, in_specs=in_specs, out_specs=out_specs, check_vma=False)
```

```python
import math

import jax
import jax.numpy as jnp
from jax import lax
from jax.experimental import pallas as pl
from jax.experimental.pallas import tpu as pltpu
from jax.sharding import PartitionSpec as P


def dft_tables(pattern):
    counter = jnp.arange(pattern, dtype=jnp.int32)
    phases = counter[:, None] * counter[None, :] % pattern
    angles = phases.astype(jnp.float32) * (2.0 * math.pi / pattern)
    factor = 1.0 / math.sqrt(pattern)
    return (
        (jnp.cos(angles) * factor).astype(jnp.bfloat16),
        (-jnp.sin(angles) * factor).astype(jnp.bfloat16),
    )


def neighbour_pairs(size, step):
    if step > 0:
        return [(i, i + 1) for i in range(size - 1)]
    return [(i + 1, i) for i in range(size - 1)]


def mode_pairs():
    n = lax.axis_size("mode")
    chips = n // 2
    core = [(i, i ^ 1) for i in range(n)]
    near = [(i, i ^ 2) for i in range(n)]
    far = [(i, 2 * (chips - 1 - i // 2) + i % 2) for i in range(n)]
    return core, near, far


def allreduce_chips(qa, qb):
    _, near, far = mode_pairs()
    qa = qa + lax.ppermute(qa, "mode", near)
    qb = qb + lax.ppermute(qb, "mode", far)
    qa = qa + lax.ppermute(qa, "mode", far)
    qb = qb + lax.ppermute(qb, "mode", near)
    return qa, qb


def reduce_scatter_mode(x):
    core_pairs, near, far = mode_pairs()
    n = lax.axis_size("mode")
    m = lax.axis_index("mode")
    c, rows, w = x.shape
    x = x.reshape(c, 2, 2, 2, rows // n, w)
    for pairs, dim, d in ((core_pairs, 3, 1), (far, 1, 4), (near, 1, 2)):
        bit = (m // d) % 2
        keep = lax.dynamic_index_in_dim(x, bit, axis=dim, keepdims=False)
        send = lax.dynamic_index_in_dim(x, 1 - bit, axis=dim, keepdims=False)
        x = keep + lax.ppermute(send, "mode", pairs)
    return x.reshape(c, rows // n, w)


def _dot(a, b):
    return jnp.dot(a, b, preferred_element_type=jnp.float32)


def _window(ext_ref, k, r, c, pat):
    width = ext_ref.shape[2]
    base = pl.multiple_of((r // 8) * 8, 8)
    span = pat + 8
    down = (span - (r - base)) % span
    rows = pltpu.roll(ext_ref[k, pl.ds(base, span), :], down, 0)[:pat]
    return pltpu.roll(rows, (width - c) % width, 1)[:, :pat]


def _place(ref, a, r, c):
    pat = a.shape[0]
    width = ref.shape[-1]
    base = pl.multiple_of((r // 8) * 8, 8)
    span = pat + 8
    wide = pltpu.roll(jnp.concatenate([a, jnp.zeros((pat, width - pat), jnp.float32)], axis=1), c, 1)
    tall = jnp.concatenate([wide, jnp.zeros((span - pat, width), jnp.float32)], axis=0)
    ref[pl.ds(base, span), :] += pltpu.roll(tall, r - base, 0)


def forward_kernel(roff, coff, cnt, core, before_ref, own_ref, after_ref, pa_ref, pb_ref, fr_ref, fi_ref,
                   exit_ref, wave_ref, power_a_ref, power_b_ref, ext_ref):
    i = pl.program_id(0)
    slots = roff.shape[0]
    pat = pa_ref.shape[1]
    band = own_ref.shape[1]
    g = core[0] + 2 * i
    gi = jnp.minimum(g, slots - 1)
    live = g < cnt[0]

    def store_power(value):
        @pl.when(i == 0)
        def _():
            power_a_ref[...] = value

        @pl.when(i == 1)
        def _():
            power_b_ref[...] = value

    @pl.when(i == 0)
    def _():
        ext_ref[:, :band, :] = before_ref[...]
        ext_ref[:, band : 2 * band, :] = own_ref[...]
        ext_ref[:, 2 * band :, :] = after_ref[...]

    @pl.when(live)
    def _():
        r = roff[gi]
        c = coff[gi]
        obj_re = _window(ext_ref, 0, r, c, pat)
        obj_im = _window(ext_ref, 1, r, c, pat)
        fr = fr_ref[...]
        fi = fi_ref[...]
        total = None
        for k, p_ref in enumerate((pa_ref, pb_ref)):
            p_re = p_ref[0]
            p_im = p_ref[1]
            e_re = (p_re * obj_re - p_im * obj_im).astype(jnp.bfloat16)
            e_im = (p_re * obj_im + p_im * obj_re).astype(jnp.bfloat16)
            h_re = (_dot(fr, e_re) - _dot(fi, e_im)).astype(jnp.bfloat16)
            h_im = (_dot(fr, e_im) + _dot(fi, e_re)).astype(jnp.bfloat16)
            v_re = _dot(h_re, fr) - _dot(h_im, fi)
            v_im = _dot(h_re, fi) + _dot(h_im, fr)
            exit_ref[0, k, 0] = e_re
            exit_ref[0, k, 1] = e_im
            wave_ref[0, k, 0] = h_re
            wave_ref[0, k, 1] = h_im
            part = v_re * v_re + v_im * v_im
            total = part if total is None else total + part
        store_power(total)

    @pl.when(g == slots)
    def _():
        total = None
        for p_ref in (pa_ref, pb_ref):
            p_re = p_ref[0]
            p_im = p_ref[1]
            part = p_re * p_re + p_im * p_im
            total = part if total is None else total + part
        store_power(total)

    @pl.when(jnp.logical_and(jnp.logical_not(live), g != slots))
    def _():
        store_power(jnp.zeros((pat, pat), jnp.float32))


def backward_kernel(roff, coff, cnt, core, exit_ref, wave_ref, ma_ref, mb_ref, meas_ref, pa_ref, pb_ref,
                    fr_ref, fi_ref, keep_ref, message_ref, own_illum_ref, numer_ref, illum_ref):
    i = pl.program_id(0)
    last = pl.num_programs(0) - 1
    slots = roff.shape[0]
    g = core[0] + 2 * i
    gi = jnp.minimum(g, slots - 1)

    @pl.when(i == 0)
    def _():
        numer_ref[...] = jnp.zeros(numer_ref.shape, jnp.float32)
        illum_ref[...] = jnp.zeros(illum_ref.shape, jnp.float32)

    @pl.when(g < cnt[0])
    def _():
        r = roff[gi]
        c = coff[gi]
        model = jnp.where(i == 0, ma_ref[...], mb_ref[...])
        scaling = jnp.sqrt(meas_ref[0]) / jnp.maximum(jnp.sqrt(model), 1.0)
        fr = fr_ref[...]
        fi = fi_ref[...]
        n_re = None
        n_im = None
        for k, p_ref in enumerate((pa_ref, pb_ref)):
            h_re = wave_ref[0, k, 0]
            h_im = wave_ref[0, k, 1]
            v_re = _dot(h_re, fr) - _dot(h_im, fi)
            v_im = _dot(h_re, fi) + _dot(h_im, fr)
            x_re = (scaling * v_re).astype(jnp.bfloat16)
            x_im = (scaling * v_im).astype(jnp.bfloat16)
            b_re = (_dot(fr, x_re) + _dot(fi, x_im)).astype(jnp.bfloat16)
            b_im = (_dot(fr, x_im) - _dot(fi, x_re)).astype(jnp.bfloat16)
            d_re = _dot(b_re, fr) + _dot(b_im, fi) - exit_ref[0, k, 0].astype(jnp.float32)
            d_im = _dot(b_im, fr) - _dot(b_re, fi) - exit_ref[0, k, 1].astype(jnp.float32)
            p_re = p_ref[0]
            p_im = p_ref[1]
            t_re = p_re * d_re + p_im * d_im
            t_im = p_re * d_im - p_im * d_re
            n_re = t_re if n_re is None else n_re + t_re
            n_im = t_im if n_im is None else n_im + t_im
        _place(numer_ref.at[0], n_re, r, c)
        _place(numer_ref.at[1], n_im, r, c)

    @pl.when(jnp.logical_and(core[0] == 1, i == last))
    def _():
        for slot in range(slots):
            @pl.when(slot < cnt[0])
            def _():
                _place(illum_ref, mb_ref[...], roff[slot], coff[slot])

    @pl.when(i == last)
    def _():
        side = core[0]
        mode = core[1]
        partner = mode + 1 - 2 * side
        band = numer_ref.shape[1] // 3
        share = band // 8
        quads = 4
        for ch in range(2):
            for b in range(3):
                for q in range(quads):
                    dst = ((ch * 3 + b) * quads + q) * share
                    kept = pl.multiple_of(b * band + (2 * q + side) * share, 8)
                    sent = pl.multiple_of(b * band + (2 * q + 1 - side) * share, 8)
                    keep_ref[dst : dst + share, :] = numer_ref[ch, pl.ds(kept, share), :]
                    message_ref[dst : dst + share, :] = numer_ref[ch, pl.ds(sent, share), :]
        top = 2 * 3 * quads * share
        for b in range(3):
            theirs = pl.multiple_of(b * band + partner * share, 8)
            mine = pl.multiple_of(b * band + mode * share, 8)
            message_ref[top + b * share : top + (b + 1) * share, :] = illum_ref[pl.ds(theirs, share), :]
            own_illum_ref[b * share : (b + 1) * share, :] = illum_ref[pl.ds(mine, share), :]


def run_forward(before, own, after, pa, pb, fr, fi, roff, coff, cnt, core):
    slots = roff.shape[0]
    local = (slots + 1) // 2
    pat = pa.shape[1]
    whole3 = lambda i, *_: (0, 0, 0)
    whole2 = lambda i, *_: (0, 0)
    per5 = lambda i, *_: (i, 0, 0, 0, 0)
    flops = local * 2 * 8 * 2 * pat ** 3
    ext_shape = (2, 3 * own.shape[1], own.shape[2])
    return pl.pallas_call(
        forward_kernel,
        grid_spec=pltpu.PrefetchScalarGridSpec(
            num_scalar_prefetch=4,
            grid=(local,),
            in_specs=[
                pl.BlockSpec(before.shape, whole3),
                pl.BlockSpec(own.shape, whole3),
                pl.BlockSpec(after.shape, whole3),
                pl.BlockSpec(pa.shape, whole3),
                pl.BlockSpec(pb.shape, whole3),
                pl.BlockSpec(fr.shape, whole2),
                pl.BlockSpec(fi.shape, whole2),
            ],
            out_specs=[
                pl.BlockSpec((1, 2, 2, pat, pat), per5),
                pl.BlockSpec((1, 2, 2, pat, pat), per5),
                pl.BlockSpec((pat, pat), whole2),
                pl.BlockSpec((pat, pat), whole2),
            ],
            scratch_shapes=[pltpu.VMEM(ext_shape, jnp.float32)],
        ),
        out_shape=[
            jax.ShapeDtypeStruct((local, 2, 2, pat, pat), jnp.bfloat16),
            jax.ShapeDtypeStruct((local, 2, 2, pat, pat), jnp.bfloat16),
            jax.ShapeDtypeStruct((pat, pat), jnp.float32),
            jax.ShapeDtypeStruct((pat, pat), jnp.float32),
        ],
        compiler_params=pltpu.CompilerParams(dimension_semantics=("arbitrary",)),
        cost_estimate=pl.CostEstimate(flops=flops, transcendentals=0, bytes_accessed=10 * 1024 * 1024),
    )(roff, coff, cnt, core, before, own, after, pa, pb, fr, fi)


def run_backward(exits, waves, model_a, model_b, measured, pa, pb, fr, fi, roff, coff, cnt, ids,
                 ext_rows, width):
    slots = roff.shape[0]
    local = (slots + 1) // 2
    pat = pa.shape[1]
    share = ext_rows // 3 // 8
    kept_rows = 2 * ext_rows // 2
    whole3 = lambda i, *_: (0, 0, 0)
    whole2 = lambda i, *_: (0, 0)
    per5 = lambda i, *_: (i, 0, 0, 0, 0)
    slot_of = lambda i, roff, coff, cnt, core: (jnp.minimum(core[0] + 2 * i, slots - 1), 0, 0)
    flops = local * 2 * 8 * 2 * pat ** 3
    return pl.pallas_call(
        backward_kernel,
        grid_spec=pltpu.PrefetchScalarGridSpec(
            num_scalar_prefetch=4,
            grid=(local,),
            in_specs=[
                pl.BlockSpec((1, 2, 2, pat, pat), per5),
                pl.BlockSpec((1, 2, 2, pat, pat), per5),
                pl.BlockSpec((pat, pat), whole2),
                pl.BlockSpec((pat, pat), whole2),
                pl.BlockSpec((1, pat, pat), slot_of),
                pl.BlockSpec(pa.shape, whole3),
                pl.BlockSpec(pb.shape, whole3),
                pl.BlockSpec(fr.shape, whole2),
                pl.BlockSpec(fi.shape, whole2),
            ],
            out_specs=[
                pl.BlockSpec((kept_rows, width), whole2),
                pl.BlockSpec((kept_rows + 3 * share, width), whole2),
                pl.BlockSpec((3 * share, width), whole2),
            ],
            scratch_shapes=[
                pltpu.VMEM((2, ext_rows, width), jnp.float32),
                pltpu.VMEM((ext_rows, width), jnp.float32),
            ],
        ),
        out_shape=[
            jax.ShapeDtypeStruct((kept_rows, width), jnp.float32),
            jax.ShapeDtypeStruct((kept_rows + 3 * share, width), jnp.float32),
            jax.ShapeDtypeStruct((3 * share, width), jnp.float32),
        ],
        compiler_params=pltpu.CompilerParams(dimension_semantics=("arbitrary",)),
        cost_estimate=pl.CostEstimate(flops=flops, transcendentals=0, bytes_accessed=12 * 1024 * 1024),
    )(roff, coff, cnt, ids, exits, waves, model_a, model_b, measured, pa, pb, fr, fi)


def local(object_field, probe, measured, row_offsets, col_offsets, tile_counts):
    rows_tile = object_field.shape[1]
    width = object_field.shape[2]
    pos_count = lax.axis_size("pos")
    mode_count = lax.axis_size("mode")
    my_mode = lax.axis_index("mode")
    share_rows = rows_tile // mode_count
    pattern = probe.shape[2]
    fr, fi = dft_tables(pattern)
    probe2 = probe[:, 0]

    core_pairs, near, far = mode_pairs()
    core = my_mode % 2
    before = lax.ppermute(object_field, "pos", neighbour_pairs(pos_count, 1))
    after = lax.ppermute(object_field, "pos", neighbour_pairs(pos_count, -1))
    partner_probe = lax.ppermute(probe2, "mode", core_pairs)
    ext_rows = 3 * rows_tile

    roff = row_offsets.astype(jnp.int32)
    coff = col_offsets.astype(jnp.int32)
    cnt = tile_counts.astype(jnp.int32)
    ids = jnp.stack([core, my_mode]).astype(jnp.int32)

    exits, waves, power_a, power_b = run_forward(
        before, object_field, after, probe2, partner_probe, fr, fi, roff, coff, cnt, ids
    )
    model_a, model_b = allreduce_chips(power_a, power_b)
    kept, message, own_illum = run_backward(
        exits, waves, model_a, model_b, measured, probe2, partner_probe, fr, fi, roff, coff, cnt, ids,
        ext_rows, width
    )

    got = lax.ppermute(message, "mode", core_pairs)
    numer_rows = kept.shape[0]
    block_shape = (2, 3, 2, 2, share_rows, width)
    blocks = kept.reshape(block_shape) + got[:numer_rows].reshape(block_shape)
    own_illum = own_illum.reshape(3, share_rows, width) + got[numer_rows:].reshape(3, share_rows, width)
    band_rows = 2 * 4 * share_rows
    to_next = jnp.concatenate([blocks[:, 2].reshape(band_rows, width), own_illum[2]], axis=0)
    to_prev = jnp.concatenate([blocks[:, 0].reshape(band_rows, width), own_illum[0]], axis=0)
    from_prev = lax.ppermute(to_next, "pos", neighbour_pairs(pos_count, 1))
    from_next = lax.ppermute(to_prev, "pos", neighbour_pairs(pos_count, -1))
    tile = (
        blocks[:, 1]
        + from_prev[:band_rows].reshape(blocks[:, 1].shape)
        + from_next[:band_rows].reshape(blocks[:, 1].shape)
    )
    illum_rows = own_illum[1] + from_prev[band_rows:] + from_next[band_rows:]
    for pairs, d in ((far, 4), (near, 2)):
        bit = (my_mode // d) % 2
        keep = lax.dynamic_index_in_dim(tile, bit, axis=1, keepdims=False)
        send = lax.dynamic_index_in_dim(tile, 1 - bit, axis=1, keepdims=False)
        tile = keep + lax.ppermute(send, "mode", pairs)

    start = my_mode * share_rows
    own_rows = lax.dynamic_slice_in_dim(object_field, start, share_rows, 1)
    return own_rows + tile / (illum_rows + 1.0)


def solution(mesh):
    in_specs = (
        P(None, "pos", None),
        P(None, "mode", None, None),
        P("pos", None, None),
        P("pos"),
        P("pos"),
        P("pos"),
    )
    out_specs = P(None, ("pos", "mode"), None)
    return jax.shard_map(local, mesh=mesh, in_specs=in_specs, out_specs=out_specs, check_vma=False)
```

```python
import math

import jax
import jax.numpy as jnp
from jax import lax
from jax.experimental import pallas as pl
from jax.experimental.pallas import tpu as pltpu
from jax.sharding import PartitionSpec as P


def dft_tables(pattern):
    counter = jnp.arange(pattern, dtype=jnp.int32)
    phases = counter[:, None] * counter[None, :] % pattern
    angles = phases.astype(jnp.float32) * (2.0 * math.pi / pattern)
    factor = 1.0 / math.sqrt(pattern)
    return (
        (jnp.cos(angles) * factor).astype(jnp.bfloat16),
        (-jnp.sin(angles) * factor).astype(jnp.bfloat16),
    )


def neighbour_pairs(size, step):
    if step > 0:
        return [(i, i + 1) for i in range(size - 1)]
    return [(i + 1, i) for i in range(size - 1)]


def mode_pairs():
    n = lax.axis_size("mode")
    chips = n // 2
    core = [(i, i ^ 1) for i in range(n)]
    near = [(i, i ^ 2) for i in range(n)]
    far = [(i, 2 * (chips - 1 - i // 2) + i % 2) for i in range(n)]
    return core, near, far


def allreduce_chips(qa, qb):
    _, near, far = mode_pairs()
    qa = qa + lax.ppermute(qa, "mode", near)
    qb = qb + lax.ppermute(qb, "mode", far)
    qa = qa + lax.ppermute(qa, "mode", far)
    qb = qb + lax.ppermute(qb, "mode", near)
    return qa, qb


def reduce_scatter_mode(x):
    core_pairs, near, far = mode_pairs()
    n = lax.axis_size("mode")
    m = lax.axis_index("mode")
    c, rows, w = x.shape
    x = x.reshape(c, 2, 2, 2, rows // n, w)
    for pairs, dim, d in ((core_pairs, 3, 1), (far, 1, 4), (near, 1, 2)):
        bit = (m // d) % 2
        keep = lax.dynamic_index_in_dim(x, bit, axis=dim, keepdims=False)
        send = lax.dynamic_index_in_dim(x, 1 - bit, axis=dim, keepdims=False)
        x = keep + lax.ppermute(send, "mode", pairs)
    return x.reshape(c, rows // n, w)


def _dot(a, b):
    return jnp.dot(a, b, preferred_element_type=jnp.float32)


def _window(ext_ref, k, r, c, pat):
    width = ext_ref.shape[2]
    base = pl.multiple_of((r // 8) * 8, 8)
    span = pat + 8
    down = (span - (r - base)) % span
    rows = pltpu.roll(ext_ref[k, pl.ds(base, span), :], down, 0)[:pat]
    return pltpu.roll(rows, (width - c) % width, 1)[:, :pat]


def _place(ref, a, r, c):
    pat = a.shape[0]
    width = ref.shape[-1]
    base = pl.multiple_of((r // 8) * 8, 8)
    span = pat + 8
    wide = pltpu.roll(jnp.concatenate([a, jnp.zeros((pat, width - pat), jnp.float32)], axis=1), c, 1)
    tall = jnp.concatenate([wide, jnp.zeros((span - pat, width), jnp.float32)], axis=0)
    ref[pl.ds(base, span), :] += pltpu.roll(tall, r - base, 0)


def forward_kernel(roff, coff, cnt, core, before_ref, own_ref, after_ref, pa_ref, pb_ref, fr_ref, fi_ref,
                   exit_ref, wave_ref, power_a_ref, power_b_ref, ext_ref):
    i = pl.program_id(0)
    slots = roff.shape[0]
    pat = pa_ref.shape[1]
    band = own_ref.shape[1]
    g = core[0] + 2 * i
    gi = jnp.minimum(g, slots - 1)
    live = g < cnt[0]

    def store_power(value):
        @pl.when(i == 0)
        def _():
            power_a_ref[...] = value

        @pl.when(i == 1)
        def _():
            power_b_ref[...] = value

    @pl.when(i == 0)
    def _():
        ext_ref[:, :band, :] = before_ref[...]
        ext_ref[:, band : 2 * band, :] = own_ref[...]
        ext_ref[:, 2 * band :, :] = after_ref[...]

    @pl.when(live)
    def _():
        r = roff[gi]
        c = coff[gi]
        obj_re = _window(ext_ref, 0, r, c, pat)
        obj_im = _window(ext_ref, 1, r, c, pat)
        fr = fr_ref[...]
        fi = fi_ref[...]
        total = None
        for k, p_ref in enumerate((pa_ref, pb_ref)):
            p_re = p_ref[0]
            p_im = p_ref[1]
            e_re = (p_re * obj_re - p_im * obj_im).astype(jnp.bfloat16)
            e_im = (p_re * obj_im + p_im * obj_re).astype(jnp.bfloat16)
            h_re = (_dot(fr, e_re) - _dot(fi, e_im)).astype(jnp.bfloat16)
            h_im = (_dot(fr, e_im) + _dot(fi, e_re)).astype(jnp.bfloat16)
            v_re = _dot(h_re, fr) - _dot(h_im, fi)
            v_im = _dot(h_re, fi) + _dot(h_im, fr)
            exit_ref[0, k, 0] = e_re
            exit_ref[0, k, 1] = e_im
            wave_ref[0, k, 0] = h_re
            wave_ref[0, k, 1] = h_im
            part = v_re * v_re + v_im * v_im
            total = part if total is None else total + part
        store_power(total)

    @pl.when(g == slots)
    def _():
        total = None
        for p_ref in (pa_ref, pb_ref):
            p_re = p_ref[0]
            p_im = p_ref[1]
            part = p_re * p_re + p_im * p_im
            total = part if total is None else total + part
        store_power(total)

    @pl.when(jnp.logical_and(jnp.logical_not(live), g != slots))
    def _():
        store_power(jnp.zeros((pat, pat), jnp.float32))


def backward_kernel(roff, coff, cnt, core, exit_ref, wave_ref, ma_ref, mb_ref, meas_ref, pa_ref, pb_ref,
                    fr_ref, fi_ref, keep_ref, message_ref, own_illum_ref, numer_ref, illum_ref):
    i = pl.program_id(0)
    last = pl.num_programs(0) - 1
    slots = roff.shape[0]
    g = core[0] + 2 * i
    gi = jnp.minimum(g, slots - 1)

    @pl.when(i == 0)
    def _():
        numer_ref[...] = jnp.zeros(numer_ref.shape, jnp.float32)
        illum_ref[...] = jnp.zeros(illum_ref.shape, jnp.float32)

    @pl.when(g < cnt[0])
    def _():
        r = roff[gi]
        c = coff[gi]
        model = jnp.where(i == 0, ma_ref[...], mb_ref[...])
        scaling = jnp.sqrt(meas_ref[0]) / jnp.maximum(jnp.sqrt(model), 1.0)
        fr = fr_ref[...]
        fi = fi_ref[...]
        n_re = None
        n_im = None
        for k, p_ref in enumerate((pa_ref, pb_ref)):
            h_re = wave_ref[0, k, 0]
            h_im = wave_ref[0, k, 1]
            v_re = _dot(h_re, fr) - _dot(h_im, fi)
            v_im = _dot(h_re, fi) + _dot(h_im, fr)
            x_re = (scaling * v_re).astype(jnp.bfloat16)
            x_im = (scaling * v_im).astype(jnp.bfloat16)
            b_re = (_dot(fr, x_re) + _dot(fi, x_im)).astype(jnp.bfloat16)
            b_im = (_dot(fr, x_im) - _dot(fi, x_re)).astype(jnp.bfloat16)
            d_re = _dot(b_re, fr) + _dot(b_im, fi) - exit_ref[0, k, 0].astype(jnp.float32)
            d_im = _dot(b_im, fr) - _dot(b_re, fi) - exit_ref[0, k, 1].astype(jnp.float32)
            p_re = p_ref[0]
            p_im = p_ref[1]
            t_re = p_re * d_re + p_im * d_im
            t_im = p_re * d_im - p_im * d_re
            n_re = t_re if n_re is None else n_re + t_re
            n_im = t_im if n_im is None else n_im + t_im
        _place(numer_ref.at[0], n_re, r, c)
        _place(numer_ref.at[1], n_im, r, c)

    @pl.when(jnp.logical_and(core[0] == 1, i == last))
    def _():
        for slot in range(slots):
            @pl.when(slot < cnt[0])
            def _():
                _place(illum_ref, mb_ref[...], roff[slot], coff[slot])

    @pl.when(i == last)
    def _():
        side = core[0]
        mode = core[1]
        partner = mode + 1 - 2 * side
        band = numer_ref.shape[1] // 3
        share = band // 8
        quads = 4
        for ch in range(2):
            for b in range(3):
                for q in range(quads):
                    dst = ((ch * 3 + b) * quads + q) * share
                    kept = pl.multiple_of(b * band + (2 * q + side) * share, 8)
                    sent = pl.multiple_of(b * band + (2 * q + 1 - side) * share, 8)
                    keep_ref[dst : dst + share, :] = numer_ref[ch, pl.ds(kept, share), :]
                    message_ref[dst : dst + share, :] = numer_ref[ch, pl.ds(sent, share), :]
        top = 2 * 3 * quads * share
        for b in range(3):
            theirs = pl.multiple_of(b * band + partner * share, 8)
            mine = pl.multiple_of(b * band + mode * share, 8)
            message_ref[top + b * share : top + (b + 1) * share, :] = illum_ref[pl.ds(theirs, share), :]
            own_illum_ref[b * share : (b + 1) * share, :] = illum_ref[pl.ds(mine, share), :]


def run_forward(before, own, after, pa, pb, fr, fi, roff, coff, cnt, core):
    slots = roff.shape[0]
    local = (slots + 1) // 2
    pat = pa.shape[1]
    whole3 = lambda i, *_: (0, 0, 0)
    whole2 = lambda i, *_: (0, 0)
    per5 = lambda i, *_: (i, 0, 0, 0, 0)
    flops = local * 2 * 8 * 2 * pat ** 3
    ext_shape = (2, 3 * own.shape[1], own.shape[2])
    return pl.pallas_call(
        forward_kernel,
        grid_spec=pltpu.PrefetchScalarGridSpec(
            num_scalar_prefetch=4,
            grid=(local,),
            in_specs=[
                pl.BlockSpec(before.shape, whole3),
                pl.BlockSpec(own.shape, whole3),
                pl.BlockSpec(after.shape, whole3),
                pl.BlockSpec(pa.shape, whole3),
                pl.BlockSpec(pb.shape, whole3),
                pl.BlockSpec(fr.shape, whole2),
                pl.BlockSpec(fi.shape, whole2),
            ],
            out_specs=[
                pl.BlockSpec((1, 2, 2, pat, pat), per5),
                pl.BlockSpec((1, 2, 2, pat, pat), per5),
                pl.BlockSpec((pat, pat), whole2),
                pl.BlockSpec((pat, pat), whole2),
            ],
            scratch_shapes=[pltpu.VMEM(ext_shape, jnp.float32)],
        ),
        out_shape=[
            jax.ShapeDtypeStruct((local, 2, 2, pat, pat), jnp.bfloat16),
            jax.ShapeDtypeStruct((local, 2, 2, pat, pat), jnp.bfloat16),
            jax.ShapeDtypeStruct((pat, pat), jnp.float32),
            jax.ShapeDtypeStruct((pat, pat), jnp.float32),
        ],
        compiler_params=pltpu.CompilerParams(dimension_semantics=("arbitrary",)),
        cost_estimate=pl.CostEstimate(flops=flops, transcendentals=0, bytes_accessed=10 * 1024 * 1024),
    )(roff, coff, cnt, core, before, own, after, pa, pb, fr, fi)


def run_backward(exits, waves, model_a, model_b, measured, pa, pb, fr, fi, roff, coff, cnt, ids,
                 ext_rows, width):
    slots = roff.shape[0]
    local = (slots + 1) // 2
    pat = pa.shape[1]
    share = ext_rows // 3 // 8
    kept_rows = 2 * ext_rows // 2
    whole3 = lambda i, *_: (0, 0, 0)
    whole2 = lambda i, *_: (0, 0)
    per5 = lambda i, *_: (i, 0, 0, 0, 0)
    slot_of = lambda i, roff, coff, cnt, core: (jnp.minimum(core[0] + 2 * i, slots - 1), 0, 0)
    flops = local * 2 * 8 * 2 * pat ** 3
    return pl.pallas_call(
        backward_kernel,
        grid_spec=pltpu.PrefetchScalarGridSpec(
            num_scalar_prefetch=4,
            grid=(local,),
            in_specs=[
                pl.BlockSpec((1, 2, 2, pat, pat), per5),
                pl.BlockSpec((1, 2, 2, pat, pat), per5),
                pl.BlockSpec((pat, pat), whole2),
                pl.BlockSpec((pat, pat), whole2),
                pl.BlockSpec((1, pat, pat), slot_of),
                pl.BlockSpec(pa.shape, whole3),
                pl.BlockSpec(pb.shape, whole3),
                pl.BlockSpec(fr.shape, whole2),
                pl.BlockSpec(fi.shape, whole2),
            ],
            out_specs=[
                pl.BlockSpec((kept_rows, width), whole2),
                pl.BlockSpec((kept_rows + 3 * share, width), whole2),
                pl.BlockSpec((3 * share, width), whole2),
            ],
            scratch_shapes=[
                pltpu.VMEM((2, ext_rows, width), jnp.float32),
                pltpu.VMEM((ext_rows, width), jnp.float32),
            ],
        ),
        out_shape=[
            jax.ShapeDtypeStruct((kept_rows, width), jnp.float32),
            jax.ShapeDtypeStruct((kept_rows + 3 * share, width), jnp.float32),
            jax.ShapeDtypeStruct((3 * share, width), jnp.float32),
        ],
        compiler_params=pltpu.CompilerParams(dimension_semantics=("arbitrary",)),
        cost_estimate=pl.CostEstimate(flops=flops, transcendentals=0, bytes_accessed=12 * 1024 * 1024),
    )(roff, coff, cnt, ids, exits, waves, model_a, model_b, measured, pa, pb, fr, fi)


def local(object_field, probe, measured, row_offsets, col_offsets, tile_counts):
    rows_tile = object_field.shape[1]
    width = object_field.shape[2]
    pos_count = lax.axis_size("pos")
    mode_count = lax.axis_size("mode")
    my_mode = lax.axis_index("mode")
    share_rows = rows_tile // mode_count
    pattern = probe.shape[2]
    fr, fi = dft_tables(pattern)
    probe2 = probe[:, 0]

    core_pairs, near, far = mode_pairs()
    core = my_mode % 2
    before = lax.ppermute(object_field, "pos", neighbour_pairs(pos_count, 1))
    after = lax.ppermute(object_field, "pos", neighbour_pairs(pos_count, -1))
    partner_probe = lax.ppermute(probe2, "mode", core_pairs)
    ext_rows = 3 * rows_tile

    roff = row_offsets.astype(jnp.int32)
    coff = col_offsets.astype(jnp.int32)
    cnt = tile_counts.astype(jnp.int32)
    ids = jnp.stack([core, my_mode]).astype(jnp.int32)

    exits, waves, power_a, power_b = run_forward(
        before, object_field, after, probe2, partner_probe, fr, fi, roff, coff, cnt, ids
    )
    model_a, model_b = allreduce_chips(power_a, power_b)
    kept, message, own_illum = run_backward(
        exits, waves, model_a, model_b, measured, probe2, partner_probe, fr, fi, roff, coff, cnt, ids,
        ext_rows, width
    )

    got = lax.ppermute(message, "mode", core_pairs)
    numer_rows = kept.shape[0]
    block_shape = (2, 3, 2, 2, share_rows, width)
    blocks = kept.reshape(block_shape) + got[:numer_rows].reshape(block_shape)
    own_illum = own_illum.reshape(3, share_rows, width) + got[numer_rows:].reshape(3, share_rows, width)
    band_rows = 2 * 4 * share_rows
    to_next = jnp.concatenate([blocks[:, 2].reshape(band_rows, width), own_illum[2]], axis=0)
    to_prev = jnp.concatenate([blocks[:, 0].reshape(band_rows, width), own_illum[0]], axis=0)
    from_prev = lax.ppermute(to_next, "pos", neighbour_pairs(pos_count, 1))
    from_next = lax.ppermute(to_prev, "pos", neighbour_pairs(pos_count, -1))
    tile = (
        blocks[:, 1]
        + from_prev[:band_rows].reshape(blocks[:, 1].shape)
        + from_next[:band_rows].reshape(blocks[:, 1].shape)
    )
    illum_rows = own_illum[1] + from_prev[band_rows:] + from_next[band_rows:]
    chip = my_mode // 2
    hi = chip // 2
    lo = chip % 2
    across = [(i, i ^ 4) for i in range(mode_count)]

    def block(a, b):
        rows = lax.dynamic_index_in_dim(tile, a, axis=1, keepdims=False)
        return lax.dynamic_index_in_dim(rows, b, axis=1, keepdims=False)

    from_near = lax.ppermute(block(hi, 1 - lo), "mode", near)
    from_far = lax.ppermute(block(1 - hi, 1 - lo), "mode", far)
    from_across = lax.ppermute(block(1 - hi, lo), "mode", across)
    tile = block(hi, lo) + from_near + from_far + from_across

    start = my_mode * share_rows
    own_rows = lax.dynamic_slice_in_dim(object_field, start, share_rows, 1)
    return own_rows + tile / (illum_rows + 1.0)


def solution(mesh):
    in_specs = (
        P(None, "pos", None),
        P(None, "mode", None, None),
        P("pos", None, None),
        P("pos"),
        P("pos"),
        P("pos"),
    )
    out_specs = P(None, ("pos", "mode"), None)
    return jax.shard_map(local, mesh=mesh, in_specs=in_specs, out_specs=out_specs, check_vma=False)
```

```python
import math

import jax
import jax.numpy as jnp
from jax import lax
from jax.experimental import pallas as pl
from jax.experimental.pallas import tpu as pltpu
from jax.sharding import PartitionSpec as P


def dft_tables(pattern):
    counter = jnp.arange(pattern, dtype=jnp.int32)
    phases = counter[:, None] * counter[None, :] % pattern
    angles = phases.astype(jnp.float32) * (2.0 * math.pi / pattern)
    factor = 1.0 / math.sqrt(pattern)
    return (
        (jnp.cos(angles) * factor).astype(jnp.bfloat16),
        (-jnp.sin(angles) * factor).astype(jnp.bfloat16),
    )


def neighbour_pairs(size, step):
    if step > 0:
        return [(i, i + 1) for i in range(size - 1)]
    return [(i + 1, i) for i in range(size - 1)]


def mode_pairs():
    n = lax.axis_size("mode")
    chips = n // 2
    core = [(i, i ^ 1) for i in range(n)]
    near = [(i, i ^ 2) for i in range(n)]
    far = [(i, 2 * (chips - 1 - i // 2) + i % 2) for i in range(n)]
    return core, near, far


def allreduce_chips(qa, qb):
    _, near, far = mode_pairs()
    qa = qa + lax.ppermute(qa, "mode", near)
    qb = qb + lax.ppermute(qb, "mode", far)
    qa = qa + lax.ppermute(qa, "mode", far)
    qb = qb + lax.ppermute(qb, "mode", near)
    return qa, qb


def reduce_scatter_mode(x):
    core_pairs, near, far = mode_pairs()
    n = lax.axis_size("mode")
    m = lax.axis_index("mode")
    c, rows, w = x.shape
    x = x.reshape(c, 2, 2, 2, rows // n, w)
    for pairs, dim, d in ((core_pairs, 3, 1), (far, 1, 4), (near, 1, 2)):
        bit = (m // d) % 2
        keep = lax.dynamic_index_in_dim(x, bit, axis=dim, keepdims=False)
        send = lax.dynamic_index_in_dim(x, 1 - bit, axis=dim, keepdims=False)
        x = keep + lax.ppermute(send, "mode", pairs)
    return x.reshape(c, rows // n, w)


def _dot(a, b):
    return jnp.dot(a, b, preferred_element_type=jnp.float32)


def _window(ext_ref, k, r, c, pat):
    width = ext_ref.shape[2]
    base = pl.multiple_of((r // 8) * 8, 8)
    span = pat + 8
    down = (span - (r - base)) % span
    rows = pltpu.roll(ext_ref[k, pl.ds(base, span), :], down, 0)[:pat]
    return pltpu.roll(rows, (width - c) % width, 1)[:, :pat]


def _place(ref, a, r, c):
    pat = a.shape[0]
    width = ref.shape[-1]
    base = pl.multiple_of((r // 8) * 8, 8)
    span = pat + 8
    wide = pltpu.roll(jnp.concatenate([a, jnp.zeros((pat, width - pat), jnp.float32)], axis=1), c, 1)
    tall = jnp.concatenate([wide, jnp.zeros((span - pat, width), jnp.float32)], axis=0)
    ref[pl.ds(base, span), :] += pltpu.roll(tall, r - base, 0)


def forward_kernel(roff, coff, cnt, core, before_ref, own_ref, after_ref, pa_ref, pb_ref, fr_ref, fi_ref,
                   exit_ref, wave_ref, power_a_ref, power_b_ref, ext_ref):
    i = pl.program_id(0)
    slots = roff.shape[0]
    pat = pa_ref.shape[1]
    band = own_ref.shape[1]
    g = core[0] + 2 * i
    gi = jnp.minimum(g, slots - 1)
    live = g < cnt[0]

    def store_power(value):
        @pl.when(i == 0)
        def _():
            power_a_ref[...] = value

        @pl.when(i == 1)
        def _():
            power_b_ref[...] = value

    @pl.when(jnp.logical_and(i == 0, core[0] == 0))
    def _():
        ext_ref[:, :band, :] = before_ref[...]
        ext_ref[:, band : 2 * band, :] = own_ref[...]
        ext_ref[:, 2 * band :, :] = after_ref[...]

    @pl.when(jnp.logical_and(i == 0, core[0] == 1))
    def _():
        ext_ref[:, :band, :] = after_ref[...]
        ext_ref[:, band : 2 * band, :] = own_ref[...]
        ext_ref[:, 2 * band :, :] = before_ref[...]

    @pl.when(live)
    def _():
        r = roff[gi]
        c = coff[gi]
        obj_re = _window(ext_ref, 0, r, c, pat)
        obj_im = _window(ext_ref, 1, r, c, pat)
        fr = fr_ref[...]
        fi = fi_ref[...]
        total = None
        for k, p_ref in enumerate((pa_ref, pb_ref)):
            p_re = p_ref[0]
            p_im = p_ref[1]
            e_re = (p_re * obj_re - p_im * obj_im).astype(jnp.bfloat16)
            e_im = (p_re * obj_im + p_im * obj_re).astype(jnp.bfloat16)
            h_re = (_dot(fr, e_re) - _dot(fi, e_im)).astype(jnp.bfloat16)
            h_im = (_dot(fr, e_im) + _dot(fi, e_re)).astype(jnp.bfloat16)
            v_re = _dot(h_re, fr) - _dot(h_im, fi)
            v_im = _dot(h_re, fi) + _dot(h_im, fr)
            exit_ref[0, k, 0] = e_re
            exit_ref[0, k, 1] = e_im
            wave_ref[0, k, 0] = h_re
            wave_ref[0, k, 1] = h_im
            part = v_re * v_re + v_im * v_im
            total = part if total is None else total + part
        store_power(total)

    @pl.when(g == slots)
    def _():
        total = None
        for p_ref in (pa_ref, pb_ref):
            p_re = p_ref[0]
            p_im = p_ref[1]
            part = p_re * p_re + p_im * p_im
            total = part if total is None else total + part
        store_power(total)

    @pl.when(jnp.logical_and(jnp.logical_not(live), g != slots))
    def _():
        store_power(jnp.zeros((pat, pat), jnp.float32))


def backward_kernel(roff, coff, cnt, core, exit_ref, wave_ref, ma_ref, mb_ref, meas_ref, pa_ref, pb_ref,
                    fr_ref, fi_ref, keep_ref, message_ref, own_illum_ref, numer_ref, illum_ref):
    i = pl.program_id(0)
    last = pl.num_programs(0) - 1
    slots = roff.shape[0]
    g = core[0] + 2 * i
    gi = jnp.minimum(g, slots - 1)

    @pl.when(i == 0)
    def _():
        numer_ref[...] = jnp.zeros(numer_ref.shape, jnp.float32)
        illum_ref[...] = jnp.zeros(illum_ref.shape, jnp.float32)

    @pl.when(g < cnt[0])
    def _():
        r = roff[gi]
        c = coff[gi]
        model = jnp.where(i == 0, ma_ref[...], mb_ref[...])
        scaling = jnp.sqrt(meas_ref[0]) / jnp.maximum(jnp.sqrt(model), 1.0)
        fr = fr_ref[...]
        fi = fi_ref[...]
        n_re = None
        n_im = None
        for k, p_ref in enumerate((pa_ref, pb_ref)):
            h_re = wave_ref[0, k, 0]
            h_im = wave_ref[0, k, 1]
            v_re = _dot(h_re, fr) - _dot(h_im, fi)
            v_im = _dot(h_re, fi) + _dot(h_im, fr)
            x_re = (scaling * v_re).astype(jnp.bfloat16)
            x_im = (scaling * v_im).astype(jnp.bfloat16)
            b_re = (_dot(fr, x_re) + _dot(fi, x_im)).astype(jnp.bfloat16)
            b_im = (_dot(fr, x_im) - _dot(fi, x_re)).astype(jnp.bfloat16)
            d_re = _dot(b_re, fr) + _dot(b_im, fi) - exit_ref[0, k, 0].astype(jnp.float32)
            d_im = _dot(b_im, fr) - _dot(b_re, fi) - exit_ref[0, k, 1].astype(jnp.float32)
            p_re = p_ref[0]
            p_im = p_ref[1]
            t_re = p_re * d_re + p_im * d_im
            t_im = p_re * d_im - p_im * d_re
            n_re = t_re if n_re is None else n_re + t_re
            n_im = t_im if n_im is None else n_im + t_im
        _place(numer_ref.at[0], n_re, r, c)
        _place(numer_ref.at[1], n_im, r, c)

    @pl.when(jnp.logical_and(core[0] == 1, i == last))
    def _():
        for slot in range(slots):
            @pl.when(slot < cnt[0])
            def _():
                _place(illum_ref, mb_ref[...], roff[slot], coff[slot])

    @pl.when(i == last)
    def _():
        side = core[0]
        mode = core[1]
        partner = mode + 1 - 2 * side
        band = numer_ref.shape[1] // 3
        share = band // 8
        quads = 4
        for ch in range(2):
            for b in range(3):
                for q in range(quads):
                    dst = ((ch * 3 + b) * quads + q) * share
                    kept = pl.multiple_of(b * band + (2 * q + side) * share, 8)
                    sent = pl.multiple_of(b * band + (2 * q + 1 - side) * share, 8)
                    keep_ref[dst : dst + share, :] = numer_ref[ch, pl.ds(kept, share), :]
                    message_ref[dst : dst + share, :] = numer_ref[ch, pl.ds(sent, share), :]
        top = 2 * 3 * quads * share
        for b in range(3):
            theirs = pl.multiple_of(b * band + partner * share, 8)
            mine = pl.multiple_of(b * band + mode * share, 8)
            message_ref[top + b * share : top + (b + 1) * share, :] = illum_ref[pl.ds(theirs, share), :]
            own_illum_ref[b * share : (b + 1) * share, :] = illum_ref[pl.ds(mine, share), :]


def run_forward(before, own, after, pa, pb, fr, fi, roff, coff, cnt, core):
    slots = roff.shape[0]
    local = (slots + 1) // 2
    pat = pa.shape[1]
    whole3 = lambda i, *_: (0, 0, 0)
    whole2 = lambda i, *_: (0, 0)
    per5 = lambda i, *_: (i, 0, 0, 0, 0)
    flops = local * 2 * 8 * 2 * pat ** 3
    ext_shape = (2, 3 * own.shape[1], own.shape[2])
    return pl.pallas_call(
        forward_kernel,
        grid_spec=pltpu.PrefetchScalarGridSpec(
            num_scalar_prefetch=4,
            grid=(local,),
            in_specs=[
                pl.BlockSpec(before.shape, whole3),
                pl.BlockSpec(own.shape, whole3),
                pl.BlockSpec(after.shape, whole3),
                pl.BlockSpec(pa.shape, whole3),
                pl.BlockSpec(pb.shape, whole3),
                pl.BlockSpec(fr.shape, whole2),
                pl.BlockSpec(fi.shape, whole2),
            ],
            out_specs=[
                pl.BlockSpec((1, 2, 2, pat, pat), per5),
                pl.BlockSpec((1, 2, 2, pat, pat), per5),
                pl.BlockSpec((pat, pat), whole2),
                pl.BlockSpec((pat, pat), whole2),
            ],
            scratch_shapes=[pltpu.VMEM(ext_shape, jnp.float32)],
        ),
        out_shape=[
            jax.ShapeDtypeStruct((local, 2, 2, pat, pat), jnp.bfloat16),
            jax.ShapeDtypeStruct((local, 2, 2, pat, pat), jnp.bfloat16),
            jax.ShapeDtypeStruct((pat, pat), jnp.float32),
            jax.ShapeDtypeStruct((pat, pat), jnp.float32),
        ],
        compiler_params=pltpu.CompilerParams(dimension_semantics=("arbitrary",)),
        cost_estimate=pl.CostEstimate(flops=flops, transcendentals=0, bytes_accessed=10 * 1024 * 1024),
    )(roff, coff, cnt, core, before, own, after, pa, pb, fr, fi)


def run_backward(exits, waves, model_a, model_b, measured, pa, pb, fr, fi, roff, coff, cnt, ids,
                 ext_rows, width):
    slots = roff.shape[0]
    local = (slots + 1) // 2
    pat = pa.shape[1]
    share = ext_rows // 3 // 8
    kept_rows = 2 * ext_rows // 2
    whole3 = lambda i, *_: (0, 0, 0)
    whole2 = lambda i, *_: (0, 0)
    per5 = lambda i, *_: (i, 0, 0, 0, 0)
    slot_of = lambda i, roff, coff, cnt, core: (jnp.minimum(core[0] + 2 * i, slots - 1), 0, 0)
    flops = local * 2 * 8 * 2 * pat ** 3
    return pl.pallas_call(
        backward_kernel,
        grid_spec=pltpu.PrefetchScalarGridSpec(
            num_scalar_prefetch=4,
            grid=(local,),
            in_specs=[
                pl.BlockSpec((1, 2, 2, pat, pat), per5),
                pl.BlockSpec((1, 2, 2, pat, pat), per5),
                pl.BlockSpec((pat, pat), whole2),
                pl.BlockSpec((pat, pat), whole2),
                pl.BlockSpec((1, pat, pat), slot_of),
                pl.BlockSpec(pa.shape, whole3),
                pl.BlockSpec(pb.shape, whole3),
                pl.BlockSpec(fr.shape, whole2),
                pl.BlockSpec(fi.shape, whole2),
            ],
            out_specs=[
                pl.BlockSpec((kept_rows, width), whole2),
                pl.BlockSpec((kept_rows + 3 * share, width), whole2),
                pl.BlockSpec((3 * share, width), whole2),
            ],
            scratch_shapes=[
                pltpu.VMEM((2, ext_rows, width), jnp.float32),
                pltpu.VMEM((ext_rows, width), jnp.float32),
            ],
        ),
        out_shape=[
            jax.ShapeDtypeStruct((kept_rows, width), jnp.float32),
            jax.ShapeDtypeStruct((kept_rows + 3 * share, width), jnp.float32),
            jax.ShapeDtypeStruct((3 * share, width), jnp.float32),
        ],
        compiler_params=pltpu.CompilerParams(dimension_semantics=("arbitrary",)),
        cost_estimate=pl.CostEstimate(flops=flops, transcendentals=0, bytes_accessed=12 * 1024 * 1024),
    )(roff, coff, cnt, ids, exits, waves, model_a, model_b, measured, pa, pb, fr, fi)


def local(object_field, probe, measured, row_offsets, col_offsets, tile_counts):
    rows_tile = object_field.shape[1]
    width = object_field.shape[2]
    pos_count = lax.axis_size("pos")
    mode_count = lax.axis_size("mode")
    my_mode = lax.axis_index("mode")
    share_rows = rows_tile // mode_count
    pattern = probe.shape[2]
    fr, fi = dft_tables(pattern)
    probe2 = probe[:, 0]

    core_pairs, near, far = mode_pairs()
    core = my_mode % 2
    halo_pairs = []
    for p in range(pos_count):
        for m in range(mode_count):
            if m % 2 == 0 and p + 1 < pos_count:
                halo_pairs.append((p * mode_count + m, (p + 1) * mode_count + m))
            if m % 2 == 1 and p >= 1:
                halo_pairs.append((p * mode_count + m, (p - 1) * mode_count + m))
    fetched = lax.ppermute(object_field, ("pos", "mode"), halo_pairs)
    partner_probe = lax.ppermute(probe2, "mode", core_pairs)
    swapped = lax.ppermute(fetched, "mode", core_pairs)
    ext_rows = 3 * rows_tile

    roff = row_offsets.astype(jnp.int32)
    coff = col_offsets.astype(jnp.int32)
    cnt = tile_counts.astype(jnp.int32)
    ids = jnp.stack([core, my_mode]).astype(jnp.int32)

    exits, waves, power_a, power_b = run_forward(
        fetched, object_field, swapped, probe2, partner_probe, fr, fi, roff, coff, cnt, ids
    )
    model_a, model_b = allreduce_chips(power_a, power_b)
    kept, message, own_illum = run_backward(
        exits, waves, model_a, model_b, measured, probe2, partner_probe, fr, fi, roff, coff, cnt, ids,
        ext_rows, width
    )

    got = lax.ppermute(message, "mode", core_pairs)
    numer_rows = kept.shape[0]
    block_shape = (2, 3, 2, 2, share_rows, width)
    blocks = kept.reshape(block_shape) + got[:numer_rows].reshape(block_shape)
    own_illum = own_illum.reshape(3, share_rows, width) + got[numer_rows:].reshape(3, share_rows, width)
    band_rows = 2 * 4 * share_rows
    to_next = jnp.concatenate([blocks[:, 2].reshape(band_rows, width), own_illum[2]], axis=0)
    to_prev = jnp.concatenate([blocks[:, 0].reshape(band_rows, width), own_illum[0]], axis=0)
    from_prev = lax.ppermute(to_next, "pos", neighbour_pairs(pos_count, 1))
    from_next = lax.ppermute(to_prev, "pos", neighbour_pairs(pos_count, -1))
    tile = (
        blocks[:, 1]
        + from_prev[:band_rows].reshape(blocks[:, 1].shape)
        + from_next[:band_rows].reshape(blocks[:, 1].shape)
    )
    illum_rows = own_illum[1] + from_prev[band_rows:] + from_next[band_rows:]
    for pairs, d in ((far, 4), (near, 2)):
        bit = (my_mode // d) % 2
        keep = lax.dynamic_index_in_dim(tile, bit, axis=1, keepdims=False)
        send = lax.dynamic_index_in_dim(tile, 1 - bit, axis=1, keepdims=False)
        tile = keep + lax.ppermute(send, "mode", pairs)

    start = my_mode * share_rows
    own_rows = lax.dynamic_slice_in_dim(object_field, start, share_rows, 1)
    return own_rows + tile / (illum_rows + 1.0)


def solution(mesh):
    in_specs = (
        P(None, "pos", None),
        P(None, "mode", None, None),
        P("pos", None, None),
        P("pos"),
        P("pos"),
        P("pos"),
    )
    out_specs = P(None, ("pos", "mode"), None)
    return jax.shard_map(local, mesh=mesh, in_specs=in_specs, out_specs=out_specs, check_vma=False)
```

```python
import math

import jax
import jax.numpy as jnp
from jax import lax
from jax.experimental import pallas as pl
from jax.experimental.pallas import tpu as pltpu
from jax.sharding import PartitionSpec as P


def dft_tables(pattern):
    counter = jnp.arange(pattern, dtype=jnp.int32)
    phases = counter[:, None] * counter[None, :] % pattern
    angles = phases.astype(jnp.float32) * (2.0 * math.pi / pattern)
    factor = 1.0 / math.sqrt(pattern)
    return (
        (jnp.cos(angles) * factor).astype(jnp.bfloat16),
        (-jnp.sin(angles) * factor).astype(jnp.bfloat16),
    )


def neighbour_pairs(size, step):
    if step > 0:
        return [(i, i + 1) for i in range(size - 1)]
    return [(i + 1, i) for i in range(size - 1)]


def mode_pairs():
    n = lax.axis_size("mode")
    chips = n // 2
    core = [(i, i ^ 1) for i in range(n)]
    near = [(i, i ^ 2) for i in range(n)]
    far = [(i, 2 * (chips - 1 - i // 2) + i % 2) for i in range(n)]
    return core, near, far


def allreduce_chips(qa, qb):
    _, near, far = mode_pairs()
    qa = qa + lax.ppermute(qa, "mode", near)
    qb = qb + lax.ppermute(qb, "mode", far)
    return (qa, lax.ppermute(qa, "mode", far)), (qb, lax.ppermute(qb, "mode", near))


def reduce_scatter_mode(x):
    core_pairs, near, far = mode_pairs()
    n = lax.axis_size("mode")
    m = lax.axis_index("mode")
    c, rows, w = x.shape
    x = x.reshape(c, 2, 2, 2, rows // n, w)
    for pairs, dim, d in ((core_pairs, 3, 1), (far, 1, 4), (near, 1, 2)):
        bit = (m // d) % 2
        keep = lax.dynamic_index_in_dim(x, bit, axis=dim, keepdims=False)
        send = lax.dynamic_index_in_dim(x, 1 - bit, axis=dim, keepdims=False)
        x = keep + lax.ppermute(send, "mode", pairs)
    return x.reshape(c, rows // n, w)


def _dot(a, b):
    return jnp.dot(a, b, preferred_element_type=jnp.float32)


def _window(ext_ref, k, r, c, pat):
    width = ext_ref.shape[2]
    base = pl.multiple_of((r // 8) * 8, 8)
    span = pat + 8
    down = (span - (r - base)) % span
    rows = pltpu.roll(ext_ref[k, pl.ds(base, span), :], down, 0)[:pat]
    return pltpu.roll(rows, (width - c) % width, 1)[:, :pat]


def _place(ref, a, r, c):
    pat = a.shape[0]
    width = ref.shape[-1]
    base = pl.multiple_of((r // 8) * 8, 8)
    span = pat + 8
    wide = pltpu.roll(jnp.concatenate([a, jnp.zeros((pat, width - pat), jnp.float32)], axis=1), c, 1)
    tall = jnp.concatenate([wide, jnp.zeros((span - pat, width), jnp.float32)], axis=0)
    ref[pl.ds(base, span), :] += pltpu.roll(tall, r - base, 0)


def forward_kernel(roff, coff, cnt, core, before_ref, own_ref, after_ref, pa_ref, pb_ref, fr_ref, fi_ref,
                   exit_ref, wave_ref, power_a_ref, power_b_ref, ext_ref):
    i = pl.program_id(0)
    slots = roff.shape[0]
    pat = pa_ref.shape[1]
    band = own_ref.shape[1]
    g = core[0] + 2 * i
    gi = jnp.minimum(g, slots - 1)
    live = g < cnt[0]

    def store_power(value):
        @pl.when(i == 0)
        def _():
            power_a_ref[...] = value

        @pl.when(i == 1)
        def _():
            power_b_ref[...] = value

    @pl.when(jnp.logical_and(i == 0, core[0] == 0))
    def _():
        ext_ref[:, :band, :] = before_ref[...]
        ext_ref[:, band : 2 * band, :] = own_ref[...]
        ext_ref[:, 2 * band :, :] = after_ref[...]

    @pl.when(jnp.logical_and(i == 0, core[0] == 1))
    def _():
        ext_ref[:, :band, :] = after_ref[...]
        ext_ref[:, band : 2 * band, :] = own_ref[...]
        ext_ref[:, 2 * band :, :] = before_ref[...]

    @pl.when(live)
    def _():
        r = roff[gi]
        c = coff[gi]
        obj_re = _window(ext_ref, 0, r, c, pat)
        obj_im = _window(ext_ref, 1, r, c, pat)
        fr = fr_ref[...]
        fi = fi_ref[...]
        total = None
        for k, p_ref in enumerate((pa_ref, pb_ref)):
            p_re = p_ref[0]
            p_im = p_ref[1]
            e_re = (p_re * obj_re - p_im * obj_im).astype(jnp.bfloat16)
            e_im = (p_re * obj_im + p_im * obj_re).astype(jnp.bfloat16)
            h_re = (_dot(fr, e_re) - _dot(fi, e_im)).astype(jnp.bfloat16)
            h_im = (_dot(fr, e_im) + _dot(fi, e_re)).astype(jnp.bfloat16)
            v_re = _dot(h_re, fr) - _dot(h_im, fi)
            v_im = _dot(h_re, fi) + _dot(h_im, fr)
            exit_ref[0, k, 0] = e_re
            exit_ref[0, k, 1] = e_im
            wave_ref[0, k, 0] = h_re
            wave_ref[0, k, 1] = h_im
            part = v_re * v_re + v_im * v_im
            total = part if total is None else total + part
        store_power(total)

    @pl.when(g == slots)
    def _():
        total = None
        for p_ref in (pa_ref, pb_ref):
            p_re = p_ref[0]
            p_im = p_ref[1]
            part = p_re * p_re + p_im * p_im
            total = part if total is None else total + part
        store_power(total)

    @pl.when(jnp.logical_and(jnp.logical_not(live), g != slots))
    def _():
        store_power(jnp.zeros((pat, pat), jnp.float32))


def backward_kernel(roff, coff, cnt, core, exit_ref, wave_ref, ma_ref, ra_ref, mb_ref, rb_ref, meas_ref,
                    pa_ref, pb_ref, fr_ref, fi_ref, keep_ref, message_ref, own_illum_ref, numer_ref, illum_ref):
    i = pl.program_id(0)
    last = pl.num_programs(0) - 1
    slots = roff.shape[0]
    g = core[0] + 2 * i
    gi = jnp.minimum(g, slots - 1)

    @pl.when(i == 0)
    def _():
        numer_ref[...] = jnp.zeros(numer_ref.shape, jnp.float32)
        illum_ref[...] = jnp.zeros(illum_ref.shape, jnp.float32)

    @pl.when(g < cnt[0])
    def _():
        r = roff[gi]
        c = coff[gi]
        model = jnp.where(i == 0, ma_ref[...] + ra_ref[...], mb_ref[...] + rb_ref[...])
        scaling = jnp.sqrt(meas_ref[0]) / jnp.maximum(jnp.sqrt(model), 1.0)
        fr = fr_ref[...]
        fi = fi_ref[...]
        n_re = None
        n_im = None
        for k, p_ref in enumerate((pa_ref, pb_ref)):
            h_re = wave_ref[0, k, 0]
            h_im = wave_ref[0, k, 1]
            v_re = _dot(h_re, fr) - _dot(h_im, fi)
            v_im = _dot(h_re, fi) + _dot(h_im, fr)
            x_re = (scaling * v_re).astype(jnp.bfloat16)
            x_im = (scaling * v_im).astype(jnp.bfloat16)
            b_re = (_dot(fr, x_re) + _dot(fi, x_im)).astype(jnp.bfloat16)
            b_im = (_dot(fr, x_im) - _dot(fi, x_re)).astype(jnp.bfloat16)
            d_re = _dot(b_re, fr) + _dot(b_im, fi) - exit_ref[0, k, 0].astype(jnp.float32)
            d_im = _dot(b_im, fr) - _dot(b_re, fi) - exit_ref[0, k, 1].astype(jnp.float32)
            p_re = p_ref[0]
            p_im = p_ref[1]
            t_re = p_re * d_re + p_im * d_im
            t_im = p_re * d_im - p_im * d_re
            n_re = t_re if n_re is None else n_re + t_re
            n_im = t_im if n_im is None else n_im + t_im
        _place(numer_ref.at[0], n_re, r, c)
        _place(numer_ref.at[1], n_im, r, c)

    @pl.when(jnp.logical_and(core[0] == 1, i == last))
    def _():
        for slot in range(slots):
            @pl.when(slot < cnt[0])
            def _():
                _place(illum_ref, mb_ref[...] + rb_ref[...], roff[slot], coff[slot])

    @pl.when(i == last)
    def _():
        side = core[0]
        mode = core[1]
        partner = mode + 1 - 2 * side
        band = numer_ref.shape[1] // 3
        share = band // 8
        quads = 4
        for ch in range(2):
            for b in range(3):
                for q in range(quads):
                    dst = ((ch * 3 + b) * quads + q) * share
                    kept = pl.multiple_of(b * band + (2 * q + side) * share, 8)
                    sent = pl.multiple_of(b * band + (2 * q + 1 - side) * share, 8)
                    keep_ref[dst : dst + share, :] = numer_ref[ch, pl.ds(kept, share), :]
                    message_ref[dst : dst + share, :] = numer_ref[ch, pl.ds(sent, share), :]
        top = 2 * 3 * quads * share
        for b in range(3):
            theirs = pl.multiple_of(b * band + partner * share, 8)
            mine = pl.multiple_of(b * band + mode * share, 8)
            message_ref[top + b * share : top + (b + 1) * share, :] = illum_ref[pl.ds(theirs, share), :]
            own_illum_ref[b * share : (b + 1) * share, :] = illum_ref[pl.ds(mine, share), :]


def run_forward(before, own, after, pa, pb, fr, fi, roff, coff, cnt, core):
    slots = roff.shape[0]
    local = (slots + 1) // 2
    pat = pa.shape[1]
    whole3 = lambda i, *_: (0, 0, 0)
    whole2 = lambda i, *_: (0, 0)
    per5 = lambda i, *_: (i, 0, 0, 0, 0)
    flops = local * 2 * 8 * 2 * pat ** 3
    ext_shape = (2, 3 * own.shape[1], own.shape[2])
    return pl.pallas_call(
        forward_kernel,
        grid_spec=pltpu.PrefetchScalarGridSpec(
            num_scalar_prefetch=4,
            grid=(local,),
            in_specs=[
                pl.BlockSpec(before.shape, whole3),
                pl.BlockSpec(own.shape, whole3),
                pl.BlockSpec(after.shape, whole3),
                pl.BlockSpec(pa.shape, whole3),
                pl.BlockSpec(pb.shape, whole3),
                pl.BlockSpec(fr.shape, whole2),
                pl.BlockSpec(fi.shape, whole2),
            ],
            out_specs=[
                pl.BlockSpec((1, 2, 2, pat, pat), per5),
                pl.BlockSpec((1, 2, 2, pat, pat), per5),
                pl.BlockSpec((pat, pat), whole2),
                pl.BlockSpec((pat, pat), whole2),
            ],
            scratch_shapes=[pltpu.VMEM(ext_shape, jnp.float32)],
        ),
        out_shape=[
            jax.ShapeDtypeStruct((local, 2, 2, pat, pat), jnp.bfloat16),
            jax.ShapeDtypeStruct((local, 2, 2, pat, pat), jnp.bfloat16),
            jax.ShapeDtypeStruct((pat, pat), jnp.float32),
            jax.ShapeDtypeStruct((pat, pat), jnp.float32),
        ],
        compiler_params=pltpu.CompilerParams(dimension_semantics=("arbitrary",)),
        cost_estimate=pl.CostEstimate(flops=flops, transcendentals=0, bytes_accessed=10 * 1024 * 1024),
    )(roff, coff, cnt, core, before, own, after, pa, pb, fr, fi)


def run_backward(exits, waves, model_a, model_b, measured, pa, pb, fr, fi, roff, coff, cnt, ids,
                 ext_rows, width):
    slots = roff.shape[0]
    local = (slots + 1) // 2
    pat = pa.shape[1]
    share = ext_rows // 3 // 8
    kept_rows = 2 * ext_rows // 2
    whole3 = lambda i, *_: (0, 0, 0)
    whole2 = lambda i, *_: (0, 0)
    per5 = lambda i, *_: (i, 0, 0, 0, 0)
    slot_of = lambda i, roff, coff, cnt, core: (jnp.minimum(core[0] + 2 * i, slots - 1), 0, 0)
    flops = local * 2 * 8 * 2 * pat ** 3
    return pl.pallas_call(
        backward_kernel,
        grid_spec=pltpu.PrefetchScalarGridSpec(
            num_scalar_prefetch=4,
            grid=(local,),
            in_specs=[
                pl.BlockSpec((1, 2, 2, pat, pat), per5),
                pl.BlockSpec((1, 2, 2, pat, pat), per5),
                pl.BlockSpec((pat, pat), whole2),
                pl.BlockSpec((pat, pat), whole2),
                pl.BlockSpec((pat, pat), whole2),
                pl.BlockSpec((pat, pat), whole2),
                pl.BlockSpec((1, pat, pat), slot_of),
                pl.BlockSpec(pa.shape, whole3),
                pl.BlockSpec(pb.shape, whole3),
                pl.BlockSpec(fr.shape, whole2),
                pl.BlockSpec(fi.shape, whole2),
            ],
            out_specs=[
                pl.BlockSpec((kept_rows, width), whole2),
                pl.BlockSpec((kept_rows + 3 * share, width), whole2),
                pl.BlockSpec((3 * share, width), whole2),
            ],
            scratch_shapes=[
                pltpu.VMEM((2, ext_rows, width), jnp.float32),
                pltpu.VMEM((ext_rows, width), jnp.float32),
            ],
        ),
        out_shape=[
            jax.ShapeDtypeStruct((kept_rows, width), jnp.float32),
            jax.ShapeDtypeStruct((kept_rows + 3 * share, width), jnp.float32),
            jax.ShapeDtypeStruct((3 * share, width), jnp.float32),
        ],
        compiler_params=pltpu.CompilerParams(dimension_semantics=("arbitrary",)),
        cost_estimate=pl.CostEstimate(flops=flops, transcendentals=0, bytes_accessed=12 * 1024 * 1024),
    )(roff, coff, cnt, ids, exits, waves, *model_a, *model_b, measured, pa, pb, fr, fi)


def local(object_field, probe, measured, row_offsets, col_offsets, tile_counts):
    rows_tile = object_field.shape[1]
    width = object_field.shape[2]
    pos_count = lax.axis_size("pos")
    mode_count = lax.axis_size("mode")
    my_mode = lax.axis_index("mode")
    share_rows = rows_tile // mode_count
    pattern = probe.shape[2]
    fr, fi = dft_tables(pattern)
    probe2 = probe[:, 0]

    core_pairs, near, far = mode_pairs()
    core = my_mode % 2
    halo_pairs = []
    for p in range(pos_count):
        for m in range(mode_count):
            if m % 2 == 0 and p + 1 < pos_count:
                halo_pairs.append((p * mode_count + m, (p + 1) * mode_count + m))
            if m % 2 == 1 and p >= 1:
                halo_pairs.append((p * mode_count + m, (p - 1) * mode_count + m))
    fetched = lax.ppermute(object_field, ("pos", "mode"), halo_pairs)
    partner_probe = lax.ppermute(probe2, "mode", core_pairs)
    swapped = lax.ppermute(fetched, "mode", core_pairs)
    ext_rows = 3 * rows_tile

    roff = row_offsets.astype(jnp.int32)
    coff = col_offsets.astype(jnp.int32)
    cnt = tile_counts.astype(jnp.int32)
    ids = jnp.stack([core, my_mode]).astype(jnp.int32)

    exits, waves, power_a, power_b = run_forward(
        fetched, object_field, swapped, probe2, partner_probe, fr, fi, roff, coff, cnt, ids
    )
    model_a, model_b = allreduce_chips(power_a, power_b)
    kept, message, own_illum = run_backward(
        exits, waves, model_a, model_b, measured, probe2, partner_probe, fr, fi, roff, coff, cnt, ids,
        ext_rows, width
    )

    got = lax.ppermute(message, "mode", core_pairs)
    numer_rows = kept.shape[0]
    block_shape = (2, 3, 2, 2, share_rows, width)
    blocks = kept.reshape(block_shape) + got[:numer_rows].reshape(block_shape)
    own_illum = own_illum.reshape(3, share_rows, width) + got[numer_rows:].reshape(3, share_rows, width)
    band_rows = 2 * 4 * share_rows
    to_next = jnp.concatenate([blocks[:, 2].reshape(band_rows, width), own_illum[2]], axis=0)
    to_prev = jnp.concatenate([blocks[:, 0].reshape(band_rows, width), own_illum[0]], axis=0)
    from_prev = lax.ppermute(to_next, "pos", neighbour_pairs(pos_count, 1))
    from_next = lax.ppermute(to_prev, "pos", neighbour_pairs(pos_count, -1))
    tile = (
        blocks[:, 1]
        + from_prev[:band_rows].reshape(blocks[:, 1].shape)
        + from_next[:band_rows].reshape(blocks[:, 1].shape)
    )
    illum_rows = own_illum[1] + from_prev[band_rows:] + from_next[band_rows:]
    for pairs, d in ((far, 4), (near, 2)):
        bit = (my_mode // d) % 2
        keep = lax.dynamic_index_in_dim(tile, bit, axis=1, keepdims=False)
        send = lax.dynamic_index_in_dim(tile, 1 - bit, axis=1, keepdims=False)
        tile = keep + lax.ppermute(send, "mode", pairs)

    start = my_mode * share_rows
    own_rows = lax.dynamic_slice_in_dim(object_field, start, share_rows, 1)
    return own_rows + tile / (illum_rows + 1.0)


def solution(mesh):
    in_specs = (
        P(None, "pos", None),
        P(None, "mode", None, None),
        P("pos", None, None),
        P("pos"),
        P("pos"),
        P("pos"),
    )
    out_specs = P(None, ("pos", "mode"), None)
    return jax.shard_map(local, mesh=mesh, in_specs=in_specs, out_specs=out_specs, check_vma=False)
```

```python
import math

import jax
import ml_dtypes
import numpy as np
import jax.numpy as jnp
from jax import lax
from jax.experimental import pallas as pl
from jax.experimental.pallas import tpu as pltpu
from jax.sharding import PartitionSpec as P


def dft_tables(pattern):
    counter = np.arange(pattern, dtype=np.int32)
    phases = counter[:, None] * counter[None, :] % pattern
    angles = phases.astype(np.float32) * np.float32(2.0 * math.pi / pattern)
    factor = np.float32(1.0 / math.sqrt(pattern))
    real = (np.cos(angles) * factor).astype(np.float32).astype(ml_dtypes.bfloat16)
    imag = (-np.sin(angles) * factor).astype(np.float32).astype(ml_dtypes.bfloat16)
    return jnp.asarray(real), jnp.asarray(imag)


def neighbour_pairs(size, step):
    if step > 0:
        return [(i, i + 1) for i in range(size - 1)]
    return [(i + 1, i) for i in range(size - 1)]


def mode_pairs():
    n = lax.axis_size("mode")
    chips = n // 2
    core = [(i, i ^ 1) for i in range(n)]
    near = [(i, i ^ 2) for i in range(n)]
    far = [(i, 2 * (chips - 1 - i // 2) + i % 2) for i in range(n)]
    return core, near, far


def allreduce_chips(qa, qb):
    _, near, far = mode_pairs()
    qa = qa + lax.ppermute(qa, "mode", near)
    qb = qb + lax.ppermute(qb, "mode", far)
    return (qa, lax.ppermute(qa, "mode", far)), (qb, lax.ppermute(qb, "mode", near))


def reduce_scatter_mode(x):
    core_pairs, near, far = mode_pairs()
    n = lax.axis_size("mode")
    m = lax.axis_index("mode")
    c, rows, w = x.shape
    x = x.reshape(c, 2, 2, 2, rows // n, w)
    for pairs, dim, d in ((core_pairs, 3, 1), (far, 1, 4), (near, 1, 2)):
        bit = (m // d) % 2
        keep = lax.dynamic_index_in_dim(x, bit, axis=dim, keepdims=False)
        send = lax.dynamic_index_in_dim(x, 1 - bit, axis=dim, keepdims=False)
        x = keep + lax.ppermute(send, "mode", pairs)
    return x.reshape(c, rows // n, w)


def _dot(a, b):
    return jnp.dot(a, b, preferred_element_type=jnp.float32)


def _window(ext_ref, k, r, c, pat):
    width = ext_ref.shape[2]
    base = pl.multiple_of((r // 8) * 8, 8)
    span = pat + 8
    down = (span - (r - base)) % span
    rows = pltpu.roll(ext_ref[k, pl.ds(base, span), :], down, 0)[:pat]
    return pltpu.roll(rows, (width - c) % width, 1)[:, :pat]


def _place(ref, a, r, c):
    pat = a.shape[0]
    width = ref.shape[-1]
    base = pl.multiple_of((r // 8) * 8, 8)
    span = pat + 8
    wide = pltpu.roll(jnp.concatenate([a, jnp.zeros((pat, width - pat), jnp.float32)], axis=1), c, 1)
    tall = jnp.concatenate([wide, jnp.zeros((span - pat, width), jnp.float32)], axis=0)
    ref[pl.ds(base, span), :] += pltpu.roll(tall, r - base, 0)


def forward_kernel(roff, coff, cnt, core, before_ref, own_ref, after_ref, pa_ref, pb_ref, fr_ref, fi_ref,
                   exit_ref, wave_ref, power_a_ref, power_b_ref, ext_ref):
    i = pl.program_id(0)
    slots = roff.shape[0]
    pat = pa_ref.shape[1]
    band = own_ref.shape[1]
    g = core[0] + 2 * i
    gi = jnp.minimum(g, slots - 1)
    live = g < cnt[0]

    def store_power(value):
        @pl.when(i == 0)
        def _():
            power_a_ref[...] = value

        @pl.when(i == 1)
        def _():
            power_b_ref[...] = value

    @pl.when(jnp.logical_and(i == 0, core[0] == 0))
    def _():
        ext_ref[:, :band, :] = before_ref[...]
        ext_ref[:, band : 2 * band, :] = own_ref[...]
        ext_ref[:, 2 * band :, :] = after_ref[...]

    @pl.when(jnp.logical_and(i == 0, core[0] == 1))
    def _():
        ext_ref[:, :band, :] = after_ref[...]
        ext_ref[:, band : 2 * band, :] = own_ref[...]
        ext_ref[:, 2 * band :, :] = before_ref[...]

    @pl.when(live)
    def _():
        r = roff[gi]
        c = coff[gi]
        obj_re = _window(ext_ref, 0, r, c, pat)
        obj_im = _window(ext_ref, 1, r, c, pat)
        fr = fr_ref[...]
        fi = fi_ref[...]
        total = None
        for k, p_ref in enumerate((pa_ref, pb_ref)):
            p_re = p_ref[0]
            p_im = p_ref[1]
            e_re = (p_re * obj_re - p_im * obj_im).astype(jnp.bfloat16)
            e_im = (p_re * obj_im + p_im * obj_re).astype(jnp.bfloat16)
            h_re = (_dot(fr, e_re) - _dot(fi, e_im)).astype(jnp.bfloat16)
            h_im = (_dot(fr, e_im) + _dot(fi, e_re)).astype(jnp.bfloat16)
            v_re = _dot(h_re, fr) - _dot(h_im, fi)
            v_im = _dot(h_re, fi) + _dot(h_im, fr)
            exit_ref[0, k, 0] = e_re
            exit_ref[0, k, 1] = e_im
            wave_ref[0, k, 0] = h_re
            wave_ref[0, k, 1] = h_im
            part = v_re * v_re + v_im * v_im
            total = part if total is None else total + part
        store_power(total)

    @pl.when(g == slots)
    def _():
        total = None
        for p_ref in (pa_ref, pb_ref):
            p_re = p_ref[0]
            p_im = p_ref[1]
            part = p_re * p_re + p_im * p_im
            total = part if total is None else total + part
        store_power(total)

    @pl.when(jnp.logical_and(jnp.logical_not(live), g != slots))
    def _():
        store_power(jnp.zeros((pat, pat), jnp.float32))


def backward_kernel(roff, coff, cnt, core, exit_ref, wave_ref, ma_ref, ra_ref, mb_ref, rb_ref, meas_ref,
                    pa_ref, pb_ref, fr_ref, fi_ref, keep_ref, message_ref, own_illum_ref, numer_ref, illum_ref):
    i = pl.program_id(0)
    last = pl.num_programs(0) - 1
    slots = roff.shape[0]
    g = core[0] + 2 * i
    gi = jnp.minimum(g, slots - 1)

    @pl.when(i == 0)
    def _():
        numer_ref[...] = jnp.zeros(numer_ref.shape, jnp.float32)
        illum_ref[...] = jnp.zeros(illum_ref.shape, jnp.float32)

    @pl.when(g < cnt[0])
    def _():
        r = roff[gi]
        c = coff[gi]
        model = jnp.where(i == 0, ma_ref[...] + ra_ref[...], mb_ref[...] + rb_ref[...])
        scaling = jnp.sqrt(meas_ref[0]) / jnp.maximum(jnp.sqrt(model), 1.0)
        fr = fr_ref[...]
        fi = fi_ref[...]
        n_re = None
        n_im = None
        for k, p_ref in enumerate((pa_ref, pb_ref)):
            h_re = wave_ref[0, k, 0]
            h_im = wave_ref[0, k, 1]
            v_re = _dot(h_re, fr) - _dot(h_im, fi)
            v_im = _dot(h_re, fi) + _dot(h_im, fr)
            x_re = (scaling * v_re).astype(jnp.bfloat16)
            x_im = (scaling * v_im).astype(jnp.bfloat16)
            b_re = (_dot(fr, x_re) + _dot(fi, x_im)).astype(jnp.bfloat16)
            b_im = (_dot(fr, x_im) - _dot(fi, x_re)).astype(jnp.bfloat16)
            d_re = _dot(b_re, fr) + _dot(b_im, fi) - exit_ref[0, k, 0].astype(jnp.float32)
            d_im = _dot(b_im, fr) - _dot(b_re, fi) - exit_ref[0, k, 1].astype(jnp.float32)
            p_re = p_ref[0]
            p_im = p_ref[1]
            t_re = p_re * d_re + p_im * d_im
            t_im = p_re * d_im - p_im * d_re
            n_re = t_re if n_re is None else n_re + t_re
            n_im = t_im if n_im is None else n_im + t_im
        _place(numer_ref.at[0], n_re, r, c)
        _place(numer_ref.at[1], n_im, r, c)

    @pl.when(jnp.logical_and(core[0] == 1, i == last))
    def _():
        for slot in range(slots):
            @pl.when(slot < cnt[0])
            def _():
                _place(illum_ref, mb_ref[...] + rb_ref[...], roff[slot], coff[slot])

    @pl.when(i == last)
    def _():
        side = core[0]
        mode = core[1]
        partner = mode + 1 - 2 * side
        band = numer_ref.shape[1] // 3
        share = band // 8
        quads = 4
        for ch in range(2):
            for b in range(3):
                for q in range(quads):
                    dst = ((ch * 3 + b) * quads + q) * share
                    kept = pl.multiple_of(b * band + (2 * q + side) * share, 8)
                    sent = pl.multiple_of(b * band + (2 * q + 1 - side) * share, 8)
                    keep_ref[dst : dst + share, :] = numer_ref[ch, pl.ds(kept, share), :]
                    message_ref[dst : dst + share, :] = numer_ref[ch, pl.ds(sent, share), :]
        top = 2 * 3 * quads * share
        for b in range(3):
            theirs = pl.multiple_of(b * band + partner * share, 8)
            mine = pl.multiple_of(b * band + mode * share, 8)
            message_ref[top + b * share : top + (b + 1) * share, :] = illum_ref[pl.ds(theirs, share), :]
            own_illum_ref[b * share : (b + 1) * share, :] = illum_ref[pl.ds(mine, share), :]


def run_forward(before, own, after, pa, pb, fr, fi, roff, coff, cnt, core):
    slots = roff.shape[0]
    local = (slots + 1) // 2
    pat = pa.shape[1]
    whole3 = lambda i, *_: (0, 0, 0)
    whole2 = lambda i, *_: (0, 0)
    per5 = lambda i, *_: (i, 0, 0, 0, 0)
    flops = local * 2 * 8 * 2 * pat ** 3
    ext_shape = (2, 3 * own.shape[1], own.shape[2])
    return pl.pallas_call(
        forward_kernel,
        grid_spec=pltpu.PrefetchScalarGridSpec(
            num_scalar_prefetch=4,
            grid=(local,),
            in_specs=[
                pl.BlockSpec(before.shape, whole3),
                pl.BlockSpec(own.shape, whole3),
                pl.BlockSpec(after.shape, whole3),
                pl.BlockSpec(pa.shape, whole3),
                pl.BlockSpec(pb.shape, whole3),
                pl.BlockSpec(fr.shape, whole2),
                pl.BlockSpec(fi.shape, whole2),
            ],
            out_specs=[
                pl.BlockSpec((1, 2, 2, pat, pat), per5),
                pl.BlockSpec((1, 2, 2, pat, pat), per5),
                pl.BlockSpec((pat, pat), whole2),
                pl.BlockSpec((pat, pat), whole2),
            ],
            scratch_shapes=[pltpu.VMEM(ext_shape, jnp.float32)],
        ),
        out_shape=[
            jax.ShapeDtypeStruct((local, 2, 2, pat, pat), jnp.bfloat16),
            jax.ShapeDtypeStruct((local, 2, 2, pat, pat), jnp.bfloat16),
            jax.ShapeDtypeStruct((pat, pat), jnp.float32),
            jax.ShapeDtypeStruct((pat, pat), jnp.float32),
        ],
        compiler_params=pltpu.CompilerParams(dimension_semantics=("arbitrary",)),
        cost_estimate=pl.CostEstimate(flops=flops, transcendentals=0, bytes_accessed=10 * 1024 * 1024),
    )(roff, coff, cnt, core, before, own, after, pa, pb, fr, fi)


def run_backward(exits, waves, model_a, model_b, measured, pa, pb, fr, fi, roff, coff, cnt, ids,
                 ext_rows, width):
    slots = roff.shape[0]
    local = (slots + 1) // 2
    pat = pa.shape[1]
    share = ext_rows // 3 // 8
    kept_rows = 2 * ext_rows // 2
    whole3 = lambda i, *_: (0, 0, 0)
    whole2 = lambda i, *_: (0, 0)
    per5 = lambda i, *_: (i, 0, 0, 0, 0)
    slot_of = lambda i, roff, coff, cnt, core: (jnp.minimum(core[0] + 2 * i, slots - 1), 0, 0)
    flops = local * 2 * 8 * 2 * pat ** 3
    return pl.pallas_call(
        backward_kernel,
        grid_spec=pltpu.PrefetchScalarGridSpec(
            num_scalar_prefetch=4,
            grid=(local,),
            in_specs=[
                pl.BlockSpec((1, 2, 2, pat, pat), per5),
                pl.BlockSpec((1, 2, 2, pat, pat), per5),
                pl.BlockSpec((pat, pat), whole2),
                pl.BlockSpec((pat, pat), whole2),
                pl.BlockSpec((pat, pat), whole2),
                pl.BlockSpec((pat, pat), whole2),
                pl.BlockSpec((1, pat, pat), slot_of),
                pl.BlockSpec(pa.shape, whole3),
                pl.BlockSpec(pb.shape, whole3),
                pl.BlockSpec(fr.shape, whole2),
                pl.BlockSpec(fi.shape, whole2),
            ],
            out_specs=[
                pl.BlockSpec((kept_rows, width), whole2),
                pl.BlockSpec((kept_rows + 3 * share, width), whole2),
                pl.BlockSpec((3 * share, width), whole2),
            ],
            scratch_shapes=[
                pltpu.VMEM((2, ext_rows, width), jnp.float32),
                pltpu.VMEM((ext_rows, width), jnp.float32),
            ],
        ),
        out_shape=[
            jax.ShapeDtypeStruct((kept_rows, width), jnp.float32),
            jax.ShapeDtypeStruct((kept_rows + 3 * share, width), jnp.float32),
            jax.ShapeDtypeStruct((3 * share, width), jnp.float32),
        ],
        compiler_params=pltpu.CompilerParams(dimension_semantics=("arbitrary",)),
        cost_estimate=pl.CostEstimate(flops=flops, transcendentals=0, bytes_accessed=12 * 1024 * 1024),
    )(roff, coff, cnt, ids, exits, waves, *model_a, *model_b, measured, pa, pb, fr, fi)


def local(object_field, probe, measured, row_offsets, col_offsets, tile_counts):
    rows_tile = object_field.shape[1]
    width = object_field.shape[2]
    pos_count = lax.axis_size("pos")
    mode_count = lax.axis_size("mode")
    my_mode = lax.axis_index("mode")
    share_rows = rows_tile // mode_count
    pattern = probe.shape[2]
    fr, fi = dft_tables(pattern)
    probe2 = probe[:, 0]

    core_pairs, near, far = mode_pairs()
    core = my_mode % 2
    halo_pairs = []
    for p in range(pos_count):
        for m in range(mode_count):
            if m % 2 == 0 and p + 1 < pos_count:
                halo_pairs.append((p * mode_count + m, (p + 1) * mode_count + m))
            if m % 2 == 1 and p >= 1:
                halo_pairs.append((p * mode_count + m, (p - 1) * mode_count + m))
    fetched = lax.ppermute(object_field, ("pos", "mode"), halo_pairs)
    partner_probe = lax.ppermute(probe2, "mode", core_pairs)
    swapped = lax.ppermute(fetched, "mode", core_pairs)
    ext_rows = 3 * rows_tile

    roff = row_offsets.astype(jnp.int32)
    coff = col_offsets.astype(jnp.int32)
    cnt = tile_counts.astype(jnp.int32)
    ids = jnp.stack([core, my_mode]).astype(jnp.int32)

    exits, waves, power_a, power_b = run_forward(
        fetched, object_field, swapped, probe2, partner_probe, fr, fi, roff, coff, cnt, ids
    )
    model_a, model_b = allreduce_chips(power_a, power_b)
    kept, message, own_illum = run_backward(
        exits, waves, model_a, model_b, measured, probe2, partner_probe, fr, fi, roff, coff, cnt, ids,
        ext_rows, width
    )

    got = lax.ppermute(message, "mode", core_pairs)
    numer_rows = kept.shape[0]
    block_shape = (2, 3, 2, 2, share_rows, width)
    blocks = kept.reshape(block_shape) + got[:numer_rows].reshape(block_shape)
    own_illum = own_illum.reshape(3, share_rows, width) + got[numer_rows:].reshape(3, share_rows, width)
    band_rows = 2 * 4 * share_rows
    to_next = jnp.concatenate([blocks[:, 2].reshape(band_rows, width), own_illum[2]], axis=0)
    to_prev = jnp.concatenate([blocks[:, 0].reshape(band_rows, width), own_illum[0]], axis=0)
    from_prev = lax.ppermute(to_next, "pos", neighbour_pairs(pos_count, 1))
    from_next = lax.ppermute(to_prev, "pos", neighbour_pairs(pos_count, -1))
    tile = (
        blocks[:, 1]
        + from_prev[:band_rows].reshape(blocks[:, 1].shape)
        + from_next[:band_rows].reshape(blocks[:, 1].shape)
    )
    illum_rows = own_illum[1] + from_prev[band_rows:] + from_next[band_rows:]
    for pairs, d in ((far, 4), (near, 2)):
        bit = (my_mode // d) % 2
        keep = lax.dynamic_index_in_dim(tile, bit, axis=1, keepdims=False)
        send = lax.dynamic_index_in_dim(tile, 1 - bit, axis=1, keepdims=False)
        tile = keep + lax.ppermute(send, "mode", pairs)

    start = my_mode * share_rows
    own_rows = lax.dynamic_slice_in_dim(object_field, start, share_rows, 1)
    return own_rows + tile / (illum_rows + 1.0)


def solution(mesh):
    in_specs = (
        P(None, "pos", None),
        P(None, "mode", None, None),
        P("pos", None, None),
        P("pos"),
        P("pos"),
        P("pos"),
    )
    out_specs = P(None, ("pos", "mode"), None)
    return jax.shard_map(local, mesh=mesh, in_specs=in_specs, out_specs=out_specs, check_vma=False)
```
